128 devices in a mesh: dp: 8 (over x_hi, z), tensor: 16 (over y, x_lo, core).
Axes of the slice: x: 4 (x_hi: 2, x_lo: 2; x = x_hi * 2 + x_lo), y: 4, z: 4, core: 2. Of those that a mesh axis runs over, the one named last changes fastest.
Arguments:
- tokens: bfloat16 [16384, 2048], P(('dp', 'tensor')), parts along dimension 0, may hold values from -6 to 6
- segment_ids: int32 [16384], P('dp'), parts along dimension 0, may hold values from 0 to 3, never falling along the last dimension, each value on 1 to 1024 neighbouring positions
- attention_gain: float32 [2048], replicated, may hold values from 0.1 to 1.9
- query_weight: bfloat16 [2048, 2048], P(None, 'tensor'), may hold values from -1 to 1
- key_weight: bfloat16 [2048, 2048], P(None, 'tensor'), may hold values from -1 to 1
- value_weight: bfloat16 [2048, 2048], P(None, 'tensor'), may hold values from -0.125 to 0.125
- output_weight: bfloat16 [2048, 2048], P('tensor'), may hold values from -0.125 to 0.125
- ffn_gain: float32 [2048], replicated, may hold values from 0.1 to 1.9
- shared_gate: bfloat16 [2048, 2816], P(None, 'tensor'), may hold values from -0.125 to 0.125
- shared_up: bfloat16 [2048, 2816], P(None, 'tensor'), may hold values from -0.125 to 0.125
- shared_down: bfloat16 [2816, 2048], P('tensor'), may hold values from -0.109375 to 0.109375
- expert_gate: bfloat16 [16, 2048, 1408], P('tensor'), may hold values from -0.125 to 0.125
- expert_up: bfloat16 [16, 2048, 1408], P('tensor'), may hold values from -0.125 to 0.125
- expert_down: bfloat16 [16, 1408, 2048], P('tensor'), may hold values from -0.15625 to 0.15625
- expert_ids: int32 [16384, 6], P('dp'), parts along dimension 0, may hold values from 0 to 15, all different within a row; in each aligned block of 128 rows (0 to 127, 128 to 255, ...) at most 64 rows name the same one
- gate_weights: float32 [16384, 6], P('dp'), parts along dimension 0, may hold values from 0.05 to 0.35
- page_table: int32 [128], P('dp'), parts along dimension 0, may hold values from 0 to 15, each once
Outputs:
- layer_out: bfloat16 [16384, 2048], P(('dp', 'tensor')), parts along dimension 0
- kv_pages: bfloat16 [2, 128, 128, 2048], P(None, 'dp', None, 'tensor'), parts along dimension 1
The draws below stay inside these ranges and needn't reach their ends.
There are 8 independent parts, one for each index of `dp`. The reference program is written for one: setup_inputs(seed, part) draws one part's arguments, and reference() takes and returns one part's arrays. A program takes and returns all parts, laid end to end along the dimension named above; an argument that names none is the same for every part. Nothing has to cross between parts.
Inputs may be any that keep to these rules, and one draw needn't show every extreme that they name: `segment_ids`: ids never fall along the stream; each of the 4 prompts holds 1 to 1024 tokens and one holds exactly 1024. `expert_ids`: each row names 6 different experts; within each aligned block of 128 rows (the tokens of one index of tensor) no expert is named by more than 64 rows, a bound that some block reaches. `page_table`: each cache page is named once.
All inputs are finite; a program needn't handle non-finite values.
Results may differ from the reference program's by a relative error of at most 0.02.
The reference program's roundings to bfloat16 on the way count: a program that leaves them out, or rounds other values in their place, can miss the bound.
Values may be sent and summed in bfloat16 or wider, within the bound.
No kernel may reach another device: no remote copies, remote signals or barrier semaphores. Data moves between devices by JAX's collectives and lax.ppermute only.
A program may use at most 128 MiB of HBM per device.

```python
import math
import jax
import jax.numpy as jnp
import numpy as np
from jax import lax

D = 2048
HD = 128
FF_EXP = 1408
SHARED_FF = 2816
TOP = 6
EXP_DEV = 1
PAGE = 128
PROMPTS = 4
TOK_DEV = 128
HEADS = 16
EXPERTS = 16
TOKENS = 2048
PAGES = 16
LONGEST = 1024
CAP = 64
N_TENSOR = 16


def draw_query_weight(key, part):
    drawn = jax.random.normal(jax.random.fold_in(key, 11), (D, HEADS * HD), jnp.float32) * D ** (-0.5)
    return jnp.clip(drawn, -1.0, 1.0).astype(jnp.bfloat16)


def draw_key_weight(key, part):
    drawn = jax.random.normal(jax.random.fold_in(key, 13), (D, HEADS * HD), jnp.float32) * D ** (-0.5)
    return jnp.clip(drawn, -1.0, 1.0).astype(jnp.bfloat16)


def levels(key, shape, shards, smallest, largest):
    loudness = 1.0
    for dim, parts in shards:
        steps = jax.random.uniform(jax.random.fold_in(jax.random.fold_in(key, 6), dim), (parts,), jnp.float32, smallest / len(shards), largest / len(shards))
        loudness = loudness * jnp.repeat(jnp.exp(steps), shape[dim] // parts).reshape((-1,) + (1,) * (len(shape) - 1 - dim))
    return loudness


def profile(count, total, reach, slope):
    weights = [(1 << 20) // math.isqrt(standing ** slope) + 1 for standing in range(2, count + 1)]
    spare, holding = total - reach - (count - 1), [1] * (count - 1)
    while spare > 0:
        candidates = [i for i in range(count - 1) if holding[i] < reach]
        whole, budget = sum([weights[i] for i in candidates]), spare
        for i in candidates:
            more = min(reach - holding[i], max(1, budget * weights[i] // whole), spare)
            holding[i] = holding[i] + more
            spare = spare - more
    return np.array([reach] + holding)


def uneven(own_key, number_of, total, most, skew):
    if number_of == 2:
        one = jax.random.randint(own_key, (), max(1, total - most), min(most, total - 1) + 1)
        return jnp.stack([one, total - one])
    lengths = jnp.asarray(profile(number_of, total, most, skew), jnp.int32)
    twos = (number_of - 1) // 2
    giver, receiver = lengths[1:1 + 2 * twos:2], lengths[2:2 + 2 * twos:2]
    margin = jnp.minimum(giver - 1, most - receiver)
    passed = jax.random.randint(jax.random.fold_in(own_key, 1), (twos,), 0, 1 << 20) % (margin + 1)
    lengths = lengths.at[1:1 + 2 * twos:2].set(giver - passed).at[2:2 + 2 * twos:2].set(receiver + passed)
    return lengths[jax.random.permutation(jax.random.fold_in(own_key, 2), number_of)]


def shared_out(own_key, own, number, rows, count, top, limit, slope):
    order = jax.random.permutation(own_key, count)
    packed, usual = load_shares(count, rows * top, limit, slope, True), load_shares(count, rows * top, limit, slope, False)
    places = jnp.arange(count)

    def named(sizes, rotation):
        used = int((sizes > 0).sum())
        fixed = max(1, used // 4)
        moved = fixed + (places - fixed + rotation * (used - fixed)) % max(1, count - fixed)
        return jnp.zeros((count,), jnp.int32).at[order[jnp.where(places < fixed, places, moved)]].set(jnp.asarray(sizes, jnp.int32))

    sizes = jnp.where(number % 4 == 0, named(packed, number // 4), named(usual, number - number // 4 - 1))
    mixed = jax.random.permutation(jax.random.fold_in(own, 3), count)
    giver, sink = mixed[0:count // 2 * 2:2], mixed[1:count // 2 * 2:2]
    margin = jnp.minimum(sizes[giver] - 1, limit - sizes[sink]) // 2
    margin = jnp.where((giver == order[0]) | (sink == order[0]) | (sizes[sink] == 0), 0, jnp.maximum(margin, 0))
    moved = jax.random.randint(jax.random.fold_in(own, 4), (count // 2,), 0, 1 << 20) % (margin + 1)
    sizes = sizes.at[giver].add(-moved).at[sink].add(moved)
    items = jnp.searchsorted(jnp.cumsum(sizes), jnp.arange(rows * top), side="right").astype(jnp.int32)
    listing = items.reshape(top, rows).T
    listing = listing[jax.random.permutation(jax.random.fold_in(own, 1), rows)]
    rotation = jax.random.randint(jax.random.fold_in(own, 2), (rows, 1), 0, top)
    return jnp.take_along_axis(listing, (jnp.arange(top)[None, :] + rotation) % top, axis=1)


def load_shares(amount, total, most, lean, full):
    loads = [(1 << 20) // math.isqrt(standing ** lean) + 1 for standing in range(1, amount + 1)]
    largest = most if full else min(most, max(-(-total // amount), total * loads[0] // sum(loads)))
    least = 1 if total - largest >= amount - 1 else 0
    counts, spare = [largest] + [least] * (amount - 1), total - largest - least * (amount - 1)
    while spare > 0:
        movable = [i for i in range(1, amount) if counts[i] < largest] or [i for i in range(1, amount) if counts[i] < most]
        whole, budget = sum([loads[i] for i in movable]), spare
        for i in movable:
            more = min(most - counts[i], max(1, budget * loads[i] // whole), spare)
            counts[i] = counts[i] + more
            spare = spare - more
    return np.array(counts)


def scatter_about(own_key, dims, deviation, limit, split=(), held_as=jnp.bfloat16):
    drawn = jax.random.normal(own_key, dims, jnp.float32) * deviation
    if len(split) > 0:
        drawn = levels(own_key, dims, split, -0.22, 0.18) * drawn
    return jnp.clip(drawn, min=-limit, max=limit).astype(held_as)


def setup_inputs(seed: int = 0, part: int = 0) -> dict:
    streams_of = jax.random.split(jax.random.key(seed), 18)
    part_keys = jax.random.split(jax.random.fold_in(streams_of[17], part), 18)
    tokens = scatter_about(part_keys[0], (TOKENS, D), 1.0, 6.0, ((0, 16),))
    segment_ids = jnp.searchsorted(jnp.cumsum(uneven(part_keys[1], PROMPTS, TOKENS, LONGEST, 2)), jnp.arange(TOKENS), side="right").astype(jnp.int32)
    attention_gain = jnp.clip(1.0 + 0.18 * jax.random.normal(streams_of[2], (D,), jnp.float32), 0.1, 1.9)
    query_weight = draw_query_weight(jax.random.fold_in(streams_of[17], 71), part)
    key_weight = draw_key_weight(jax.random.fold_in(streams_of[17], 71), part)
    value_weight = scatter_about(streams_of[5], (D, HEADS * HD), D ** -0.5, 0.125, ((1, 16),))
    output_weight = scatter_about(streams_of[6], (HEADS * HD, D), (HEADS * HD) ** -0.5, 0.125, ((0, 16),))
    ffn_gain = jnp.clip(1.0 + 0.18 * jax.random.normal(streams_of[7], (D,), jnp.float32), 0.1, 1.9)
    shared_gate = scatter_about(streams_of[8], (D, SHARED_FF), D ** -0.5, 0.125, ((1, 16),))
    shared_up = scatter_about(streams_of[9], (D, SHARED_FF), D ** -0.5, 0.125, ((1, 16),))
    shared_down = scatter_about(streams_of[10], (SHARED_FF, D), SHARED_FF ** -0.5, 0.109375, ((0, 16),))
    expert_gate = scatter_about(streams_of[11], (EXPERTS, D, FF_EXP), D ** -0.5, 0.125, ((0, 16),))
    expert_up = scatter_about(streams_of[12], (EXPERTS, D, FF_EXP), D ** -0.5, 0.125, ((0, 16),))
    expert_down = scatter_about(streams_of[13], (EXPERTS, FF_EXP, D), FF_EXP ** -0.5, 0.15625, ((0, 16),))
    expert_ids_keys = jax.random.split(jax.random.fold_in(part_keys[14], 1), TOKENS // TOK_DEV)
    expert_ids_turns = jax.random.permutation(jax.random.fold_in(part_keys[14], 3), TOKENS // TOK_DEV)
    expert_ids = jax.vmap(lambda own, number: shared_out(jax.random.fold_in(part_keys[14], 2), own, number, TOK_DEV, EXPERTS, TOP, CAP, 2))(expert_ids_keys, expert_ids_turns).reshape((TOKENS, TOP))
    gate_weights = jnp.clip(jax.random.uniform(part_keys[15], (TOKENS, TOP), jnp.float32, 0.05, 0.35), 0.05, 0.35)
    page_table = jax.random.permutation(part_keys[16], PAGES).astype(jnp.int32)
    return {"tokens": tokens, "segment_ids": segment_ids, "attention_gain": attention_gain, "query_weight": query_weight, "key_weight": key_weight, "value_weight": value_weight, "output_weight": output_weight, "ffn_gain": ffn_gain, "shared_gate": shared_gate, "shared_up": shared_up, "shared_down": shared_down, "expert_gate": expert_gate, "expert_up": expert_up, "expert_down": expert_down, "expert_ids": expert_ids, "gate_weights": gate_weights, "page_table": page_table}


def rms_scale(hidden, gain):
    widened = hidden.astype(jnp.float32)
    inverse = lax.rsqrt(lax.optimization_barrier(jnp.mean(widened * widened, axis=-1, keepdims=True)) + 1e-06)
    return (widened * inverse * gain).astype(jnp.bfloat16)

def attend(queries, keys, values, segment_ids):
    scale = HD ** (-0.5)
    positions = jnp.arange(TOKENS, dtype=jnp.int32)
    span = min(512, TOKENS)
    keys_wide = keys.astype(jnp.float32)
    values_wide = values.astype(jnp.float32)

    def one_block(start):
        query_rows = lax.dynamic_slice_in_dim(queries, start, span, 0).astype(jnp.float32)
        query_segments = lax.dynamic_slice_in_dim(segment_ids, start, span, 0)
        query_positions = start + jnp.arange(span, dtype=jnp.int32)
        scores = jnp.einsum('qhd,khd->hqk', query_rows, keys_wide) * scale
        allowed = (query_segments[:, None] == segment_ids[None, :]) & (positions[None, :] <= query_positions[:, None])
        scores = jnp.where(allowed[None], scores, -jnp.inf)
        highest = lax.optimization_barrier(jnp.max(scores, axis=-1, keepdims=True))
        weights = jnp.exp(scores - highest)
        probs = (weights / lax.optimization_barrier(jnp.sum(weights, axis=-1, keepdims=True))).astype(jnp.bfloat16)
        context = jnp.einsum('hqk,khd->qhd', probs.astype(jnp.float32), values_wide)
        return context.astype(jnp.bfloat16)
    starts = jnp.arange(TOKENS // span, dtype=jnp.int32) * span
    return lax.map(one_block, starts).reshape(TOKENS, HEADS * HD)

def grouped_sum(left, right):
    left_groups = left.reshape(left.shape[0], N_TENSOR, -1).transpose(1, 0, 2)
    right_groups = right.reshape(N_TENSOR, -1, right.shape[1])

    def add_group(total, pair):
        partial_product = jnp.dot(pair[0], pair[1], preferred_element_type=jnp.float32)
        rounded = lax.optimization_barrier(partial_product.astype(jnp.bfloat16))
        return (total + rounded.astype(jnp.float32), None)
    start_total = jnp.zeros((left.shape[0], right.shape[1]), jnp.float32)
    total, _ = lax.scan(add_group, start_total, (left_groups, right_groups))
    return total

def reference(tokens, segment_ids, attention_gain, query_weight, key_weight, value_weight, output_weight, ffn_gain, shared_gate, shared_up, shared_down, expert_gate, expert_up, expert_down, expert_ids, gate_weights, page_table):
    normed = rms_scale(tokens, attention_gain)
    queries = jnp.dot(normed, query_weight, preferred_element_type=jnp.float32).astype(jnp.bfloat16)
    keys = jnp.dot(normed, key_weight, preferred_element_type=jnp.float32).astype(jnp.bfloat16)
    values = jnp.dot(normed, value_weight, preferred_element_type=jnp.float32).astype(jnp.bfloat16)
    cache = jnp.stack([keys, values]).reshape(2, PAGES, PAGE, HEADS * HD)
    kv_pages = jnp.zeros_like(cache).at[:, page_table].set(cache)
    context = attend(queries.reshape(TOKENS, HEADS, HD), keys.reshape(TOKENS, HEADS, HD), values.reshape(TOKENS, HEADS, HD), segment_ids)
    attention = grouped_sum(context, output_weight)
    residual = (tokens.astype(jnp.float32) + attention).astype(jnp.bfloat16)
    normed_ffn = rms_scale(residual, ffn_gain)
    shared_hidden = (jax.nn.silu(jnp.dot(normed_ffn, shared_gate, preferred_element_type=jnp.float32)) * jnp.dot(normed_ffn, shared_up, preferred_element_type=jnp.float32)).astype(jnp.bfloat16)
    capacity = N_TENSOR * CAP
    token_index = jnp.arange(TOKENS, dtype=jnp.int32)

    def expert_term(total, expert):
        chosen = expert_ids == expert
        hits = lax.optimization_barrier(jnp.sum(chosen.astype(jnp.int32), axis=1))
        weight = lax.optimization_barrier(jnp.sum(jnp.where(chosen, gate_weights, 0.0), axis=1))
        rank = jnp.cumsum(hits) - hits
        slot = jnp.where(hits > 0, rank, capacity).astype(jnp.int32)
        slot_token = jnp.zeros((capacity,), jnp.int32).at[slot].set(token_index, mode='drop')
        slot_weight = jnp.zeros((capacity,), jnp.float32).at[slot].set(weight, mode='drop')
        picked = normed_ffn[slot_token]
        gate_part = jnp.dot(picked, expert_gate[expert], preferred_element_type=jnp.float32)
        upward = jnp.dot(picked, expert_up[expert], preferred_element_type=jnp.float32)
        hidden = (jax.nn.silu(gate_part) * upward).astype(jnp.bfloat16)
        out_rows = jnp.dot(hidden, expert_down[expert], preferred_element_type=jnp.float32).astype(jnp.bfloat16)
        return total.at[slot_token].add(slot_weight[:, None] * out_rows.astype(jnp.float32))
    hidden_groups = shared_hidden.reshape(TOKENS, N_TENSOR, -1).transpose(1, 0, 2)
    down_groups = shared_down.reshape(N_TENSOR, -1, D)

    def add_group(total, item):
        group, hidden_part, down_part = item
        partial_sum = jnp.dot(hidden_part, down_part, preferred_element_type=jnp.float32)
        for local in range(EXP_DEV):
            partial_sum = expert_term(partial_sum, (group * EXP_DEV + local).astype(jnp.int32))
        rounded = lax.optimization_barrier(partial_sum.astype(jnp.bfloat16))
        return (total + rounded.astype(jnp.float32), None)
    ffn_out, _ = lax.scan(add_group, jnp.zeros((TOKENS, D), jnp.float32), (jnp.arange(N_TENSOR, dtype=jnp.int32), hidden_groups, down_groups))
    layer_out = (residual.astype(jnp.float32) + ffn_out).astype(jnp.bfloat16)
    return (layer_out, kv_pages)
```

```python
import jax
import jax.numpy as jnp
from jax import lax
from jax.sharding import PartitionSpec as P

HD = 128
TOP = 6
PAGE = 128


def rms_scale(hidden, gain):
    widened = hidden.astype(jnp.float32)
    inverse = lax.rsqrt(jnp.mean(widened * widened, axis=-1, keepdims=True) + 1e-06)
    return (widened * inverse * gain).astype(jnp.bfloat16)


def attend(projected, segment_ids, head_count):
    total_tokens = projected.shape[0]
    inner = head_count * HD
    queries = projected[:, :inner].reshape(total_tokens, head_count, HD)
    keys = projected[:, inner : 2 * inner].reshape(total_tokens, head_count, HD)
    values = projected[:, 2 * inner :].reshape(total_tokens, head_count, HD)
    scale = HD ** (-0.5)
    positions = jnp.arange(total_tokens, dtype=jnp.int32)
    span = min(512, total_tokens)

    def one_block(start):
        query_rows = lax.dynamic_slice_in_dim(queries, start, span, 0)
        query_segments = lax.dynamic_slice_in_dim(segment_ids, start, span, 0)
        query_positions = start + jnp.arange(span, dtype=jnp.int32)
        scores = (
            jnp.einsum("qhd,khd->hqk", query_rows, keys, preferred_element_type=jnp.float32) * scale
        )
        allowed = (query_segments[:, None] == segment_ids[None, :]) & (
            positions[None, :] <= query_positions[:, None]
        )
        scores = jnp.where(allowed[None], scores, -jnp.inf)
        highest = jnp.max(scores, axis=-1, keepdims=True)
        weights = jnp.exp(scores - highest)
        probs = (weights / jnp.sum(weights, axis=-1, keepdims=True)).astype(jnp.bfloat16)
        context = jnp.einsum("hqk,khd->qhd", probs, values, preferred_element_type=jnp.float32)
        return context.astype(jnp.bfloat16)

    starts = jnp.arange(total_tokens // span, dtype=jnp.int32) * span
    context = lax.map(one_block, starts).reshape(total_tokens, inner)
    return (context, keys.reshape(total_tokens, inner), values.reshape(total_tokens, inner))


def expert_apply(picked, gate_w, up_w, down_w):
    gate_part = jnp.dot(picked, gate_w, preferred_element_type=jnp.float32)
    upward = jnp.dot(picked, up_w, preferred_element_type=jnp.float32)
    hidden = (jax.nn.silu(gate_part) * upward).astype(jnp.bfloat16)
    return jnp.dot(hidden, down_w, preferred_element_type=jnp.float32).astype(jnp.bfloat16)


def shards(
    tokens,
    segment_ids,
    attention_gain,
    query_weight,
    key_weight,
    value_weight,
    output_weight,
    ffn_gain,
    shared_gate,
    shared_up,
    shared_down,
    expert_gate,
    expert_up,
    expert_down,
    expert_ids,
    gate_weights,
    page_table,
):
    tok_dev = tokens.shape[0]
    groups = lax.axis_size("tensor")
    position = lax.axis_index("tensor")
    inner = query_weight.shape[1]
    head_count = inner // HD
    model_width = tokens.shape[1]

    projection = jnp.concatenate([query_weight, key_weight, value_weight], axis=1)
    normed_all = lax.all_gather(rms_scale(tokens, attention_gain), "tensor", axis=0, tiled=True)
    out_weight_all = lax.all_gather(output_weight, "tensor", axis=0, tiled=True)
    projected = jnp.dot(normed_all, projection, preferred_element_type=jnp.float32).astype(
        jnp.bfloat16
    )
    context, keys, values = attend(projected, segment_ids, head_count)
    cache = jnp.stack([keys, values]).reshape(2, -1, PAGE, inner)
    kv_pages = jnp.zeros_like(cache).at[:, page_table].set(cache)

    received = lax.all_to_all(
        context.reshape(groups, tok_dev, inner), "tensor", split_axis=0, concat_axis=0, tiled=True
    )
    partials = jnp.einsum(
        "gtd,gdo->gto",
        received,
        out_weight_all.reshape(groups, inner, model_width),
        preferred_element_type=jnp.float32,
    ).astype(jnp.bfloat16)
    attention = jnp.sum(partials.astype(jnp.float32), axis=0)
    residual = (tokens.astype(jnp.float32) + attention).astype(jnp.bfloat16)
    normed_ffn = rms_scale(residual, ffn_gain)
    normed_stream = lax.all_gather(normed_ffn, "tensor", axis=0, tiled=True)

    shared_columns = jnp.concatenate([shared_gate, shared_up], axis=1)
    shared_width = shared_gate.shape[1]
    joined = jnp.dot(normed_stream, shared_columns, preferred_element_type=jnp.float32)
    hidden_all = (jax.nn.silu(joined[:, :shared_width]) * joined[:, shared_width:]).astype(
        jnp.bfloat16
    )
    term = jnp.dot(hidden_all, shared_down, preferred_element_type=jnp.float32)

    local_experts = expert_gate.shape[0]
    expert_count = local_experts * groups
    capacity = tok_dev * TOP // expert_count + tok_dev // 8
    id_blocks = expert_ids.reshape(groups, tok_dev, -1)
    gate_blocks = gate_weights.reshape(groups, tok_dev, -1)
    token_blocks = normed_stream.reshape(groups, tok_dev, model_width)
    slots = jnp.arange(capacity, dtype=jnp.int32)
    for local in range(local_experts):
        expert = position * local_experts + local
        chosen = id_blocks == expert
        hits = jnp.sum(chosen.astype(jnp.int32), axis=2)
        weight = jnp.sum(jnp.where(chosen, gate_blocks, 0.0), axis=2)
        rank = jnp.cumsum(hits, axis=1) - hits
        onehot = ((hits[:, None, :] > 0) & (rank[:, None, :] == slots[None, :, None])).astype(
            jnp.bfloat16
        )
        picked = jnp.einsum(
            "bst,btd->bsd", onehot, token_blocks, preferred_element_type=jnp.float32
        ).astype(jnp.bfloat16)
        rows = expert_apply(
            picked.reshape(-1, model_width),
            expert_gate[local],
            expert_up[local],
            expert_down[local],
        )
        back = jnp.einsum(
            "bst,bsd->btd",
            onehot,
            rows.reshape(groups, capacity, model_width),
            preferred_element_type=jnp.float32,
        )
        term = term + weight.reshape(-1, 1) * back.reshape(-1, model_width)
    ffn_out = lax.psum_scatter(
        term.astype(jnp.bfloat16), "tensor", scatter_dimension=0, tiled=True
    ).astype(jnp.float32)
    layer_out = (residual.astype(jnp.float32) + ffn_out).astype(jnp.bfloat16)
    return (layer_out, kv_pages)


def solution(mesh):
    placed = (
        P(("dp", "tensor"), None),
        P("dp"),
        P(),
        P(None, "tensor"),
        P(None, "tensor"),
        P(None, "tensor"),
        P("tensor", None),
        P(),
        P(None, "tensor"),
        P(None, "tensor"),
        P("tensor", None),
        P("tensor", None, None),
        P("tensor", None, None),
        P("tensor", None, None),
        P("dp", None),
        P("dp", None),
        P("dp"),
    )
    return jax.shard_map(
        shards,
        mesh=mesh,
        in_specs=placed,
        out_specs=(P(("dp", "tensor"), None), P(None, "dp", None, "tensor")),
        check_vma=False,
    )
```

```python
import jax
import jax.numpy as jnp
from jax import lax
from jax.sharding import PartitionSpec as P

HD = 128
TOP = 6
PAGE = 128


def rms_scale(hidden, gain):
    widened = hidden.astype(jnp.float32)
    inverse = lax.rsqrt(jnp.mean(widened * widened, axis=-1, keepdims=True) + 1e-06)
    return (widened * inverse * gain).astype(jnp.bfloat16)


def attend(projected, segment_ids, head_count):
    total_tokens = projected.shape[0]
    inner = head_count * HD
    queries = projected[:, :inner].reshape(total_tokens, head_count, HD)
    keys = projected[:, inner : 2 * inner].reshape(total_tokens, head_count, HD)
    values = projected[:, 2 * inner :].reshape(total_tokens, head_count, HD)
    scale = HD ** (-0.5)
    positions = jnp.arange(total_tokens, dtype=jnp.int32)
    span = min(512, total_tokens)

    def one_block(start):
        query_rows = lax.dynamic_slice_in_dim(queries, start, span, 0)
        query_segments = lax.dynamic_slice_in_dim(segment_ids, start, span, 0)
        query_positions = start + jnp.arange(span, dtype=jnp.int32)
        scores = (
            jnp.einsum("qhd,khd->hqk", query_rows, keys, preferred_element_type=jnp.float32) * scale
        )
        allowed = (query_segments[:, None] == segment_ids[None, :]) & (
            positions[None, :] <= query_positions[:, None]
        )
        scores = jnp.where(allowed[None], scores, -jnp.inf)
        highest = jnp.max(scores, axis=-1, keepdims=True)
        weights = jnp.exp(scores - highest)
        probs = (weights / jnp.sum(weights, axis=-1, keepdims=True)).astype(jnp.bfloat16)
        context = jnp.einsum("hqk,khd->qhd", probs, values, preferred_element_type=jnp.float32)
        return context.astype(jnp.bfloat16)

    starts = jnp.arange(total_tokens // span, dtype=jnp.int32) * span
    context = lax.map(one_block, starts).reshape(total_tokens, inner)
    return (context, keys.reshape(total_tokens, inner), values.reshape(total_tokens, inner))


def expert_apply(picked, gate_w, up_w, down_w):
    gate_part = jnp.dot(picked, gate_w, preferred_element_type=jnp.float32)
    upward = jnp.dot(picked, up_w, preferred_element_type=jnp.float32)
    hidden = (jax.nn.silu(gate_part) * upward).astype(jnp.bfloat16)
    return jnp.dot(hidden, down_w, preferred_element_type=jnp.float32).astype(jnp.bfloat16)


def ring_reduce_scatter(partial, groups):
    ring = groups // 4
    rows = partial.shape[0] // groups
    width = partial.shape[1]
    me = lax.axis_index("tensor")
    y = me // 4
    side = (me // 2) % 2
    core = me % 2
    blocks = partial.reshape(ring, 2, 2, rows, width)
    core_pairs = [(t, t ^ 1) for t in range(groups)]
    keep = lax.dynamic_index_in_dim(blocks, core, axis=2, keepdims=False)
    give = lax.dynamic_index_in_dim(blocks, 1 - core, axis=2, keepdims=False)
    got = lax.ppermute(give, "tensor", core_pairs)
    summed = keep.astype(jnp.float32) + got.astype(jnp.float32)
    half = width // 2
    forward_part = summed[..., :half]
    backward_part = summed[..., half:]
    forward_pairs = [(t, ((t // 4 + 1) % ring) * 4 + t % 4) for t in range(groups)]
    backward_pairs = [(t, ((t // 4 + ring - 1) % ring) * 4 + t % 4) for t in range(groups)]
    carry_f = lax.dynamic_index_in_dim(forward_part, (y + ring - 1) % ring, 0, False)
    carry_b = lax.dynamic_index_in_dim(backward_part, (y + 1) % ring, 0, False)
    carry_f = carry_f.astype(jnp.bfloat16)
    carry_b = carry_b.astype(jnp.bfloat16)
    for step in range(ring - 1):
        recv_f = lax.ppermute(carry_f, "tensor", forward_pairs)
        recv_b = lax.ppermute(carry_b, "tensor", backward_pairs)
        index_f = (y + 2 * ring - step - 2) % ring
        index_b = (y + step + 2) % ring
        acc_f = recv_f.astype(jnp.float32) + lax.dynamic_index_in_dim(
            forward_part, index_f, 0, False
        )
        acc_b = recv_b.astype(jnp.float32) + lax.dynamic_index_in_dim(
            backward_part, index_b, 0, False
        )
        carry_f = acc_f.astype(jnp.bfloat16)
        carry_b = acc_b.astype(jnp.bfloat16)
    mine = jnp.concatenate([acc_f, acc_b], axis=-1)
    side_pairs = [(t, t ^ 2) for t in range(groups)]
    keep_side = lax.dynamic_index_in_dim(mine, side, 0, False)
    give_side = lax.dynamic_index_in_dim(mine, 1 - side, 0, False).astype(jnp.bfloat16)
    got_side = lax.ppermute(give_side, "tensor", side_pairs)
    return keep_side + got_side.astype(jnp.float32)


def shards(
    tokens,
    segment_ids,
    attention_gain,
    query_weight,
    key_weight,
    value_weight,
    output_weight,
    ffn_gain,
    shared_gate,
    shared_up,
    shared_down,
    expert_gate,
    expert_up,
    expert_down,
    expert_ids,
    gate_weights,
    page_table,
):
    tok_dev = tokens.shape[0]
    groups = lax.axis_size("tensor")
    position = lax.axis_index("tensor")
    inner = query_weight.shape[1]
    head_count = inner // HD
    model_width = tokens.shape[1]

    projection = jnp.concatenate([query_weight, key_weight, value_weight], axis=1)
    normed_all = lax.all_gather(rms_scale(tokens, attention_gain), "tensor", axis=0, tiled=True)
    out_weight_all = lax.all_gather(output_weight, "tensor", axis=0, tiled=True)
    projected = jnp.dot(normed_all, projection, preferred_element_type=jnp.float32).astype(
        jnp.bfloat16
    )
    context, keys, values = attend(projected, segment_ids, head_count)
    cache = jnp.stack([keys, values]).reshape(2, -1, PAGE, inner)
    kv_pages = jnp.zeros_like(cache).at[:, page_table].set(cache)

    received = lax.all_to_all(
        context.reshape(groups, tok_dev, inner), "tensor", split_axis=0, concat_axis=0, tiled=True
    )
    partials = jnp.einsum(
        "gtd,gdo->gto",
        received,
        out_weight_all.reshape(groups, inner, model_width),
        preferred_element_type=jnp.float32,
    ).astype(jnp.bfloat16)
    attention = jnp.sum(partials.astype(jnp.float32), axis=0)
    residual = (tokens.astype(jnp.float32) + attention).astype(jnp.bfloat16)
    normed_ffn = rms_scale(residual, ffn_gain)
    normed_stream = lax.all_gather(normed_ffn, "tensor", axis=0, tiled=True)

    shared_columns = jnp.concatenate([shared_gate, shared_up], axis=1)
    shared_width = shared_gate.shape[1]
    joined = jnp.dot(normed_stream, shared_columns, preferred_element_type=jnp.float32)
    hidden_all = (jax.nn.silu(joined[:, :shared_width]) * joined[:, shared_width:]).astype(
        jnp.bfloat16
    )
    term = jnp.dot(hidden_all, shared_down, preferred_element_type=jnp.float32)

    local_experts = expert_gate.shape[0]
    expert_count = local_experts * groups
    capacity = tok_dev * TOP // expert_count + tok_dev // 8
    id_blocks = expert_ids.reshape(groups, tok_dev, -1)
    gate_blocks = gate_weights.reshape(groups, tok_dev, -1)
    token_blocks = normed_stream.reshape(groups, tok_dev, model_width)
    slots = jnp.arange(capacity, dtype=jnp.int32)
    for local in range(local_experts):
        expert = position * local_experts + local
        chosen = id_blocks == expert
        hits = jnp.sum(chosen.astype(jnp.int32), axis=2)
        weight = jnp.sum(jnp.where(chosen, gate_blocks, 0.0), axis=2)
        rank = jnp.cumsum(hits, axis=1) - hits
        onehot = ((hits[:, None, :] > 0) & (rank[:, None, :] == slots[None, :, None])).astype(
            jnp.bfloat16
        )
        picked = jnp.einsum(
            "bst,btd->bsd", onehot, token_blocks, preferred_element_type=jnp.float32
        ).astype(jnp.bfloat16)
        rows = expert_apply(
            picked.reshape(-1, model_width),
            expert_gate[local],
            expert_up[local],
            expert_down[local],
        )
        back = jnp.einsum(
            "bst,bsd->btd",
            onehot,
            rows.reshape(groups, capacity, model_width),
            preferred_element_type=jnp.float32,
        ).astype(jnp.bfloat16)
        term = term + weight.reshape(-1, 1) * back.reshape(-1, model_width).astype(jnp.float32)
    ffn_out = ring_reduce_scatter(term.astype(jnp.bfloat16), groups)
    layer_out = (residual.astype(jnp.float32) + ffn_out).astype(jnp.bfloat16)
    return (layer_out, kv_pages)


def solution(mesh):
    placed = (
        P(("dp", "tensor"), None),
        P("dp"),
        P(),
        P(None, "tensor"),
        P(None, "tensor"),
        P(None, "tensor"),
        P("tensor", None),
        P(),
        P(None, "tensor"),
        P(None, "tensor"),
        P("tensor", None),
        P("tensor", None, None),
        P("tensor", None, None),
        P("tensor", None, None),
        P("dp", None),
        P("dp", None),
        P("dp"),
    )
    return jax.shard_map(
        shards,
        mesh=mesh,
        in_specs=placed,
        out_specs=(P(("dp", "tensor"), None), P(None, "dp", None, "tensor")),
        check_vma=False,
    )
```

```python
import jax
import jax.numpy as jnp
from jax import lax
from jax.sharding import PartitionSpec as P

HD = 128
TOP = 6
PAGE = 128


def rms_scale(hidden, gain):
    widened = hidden.astype(jnp.float32)
    inverse = lax.rsqrt(jnp.mean(widened * widened, axis=-1, keepdims=True) + 1e-06)
    return (widened * inverse * gain).astype(jnp.bfloat16)


def attend(projected, segment_ids, head_count):
    total_tokens = projected.shape[0]
    inner = head_count * HD
    queries = projected[:, :inner].reshape(total_tokens, head_count, HD)
    keys = projected[:, inner : 2 * inner].reshape(total_tokens, head_count, HD)
    values = projected[:, 2 * inner :].reshape(total_tokens, head_count, HD)
    scale = HD ** (-0.5)
    positions = jnp.arange(total_tokens, dtype=jnp.int32)
    span = min(512, total_tokens)

    def one_block(start):
        query_rows = lax.dynamic_slice_in_dim(queries, start, span, 0)
        query_segments = lax.dynamic_slice_in_dim(segment_ids, start, span, 0)
        query_positions = start + jnp.arange(span, dtype=jnp.int32)
        scores = (
            jnp.einsum("qhd,khd->hqk", query_rows, keys, preferred_element_type=jnp.float32) * scale
        )
        allowed = (query_segments[:, None] == segment_ids[None, :]) & (
            positions[None, :] <= query_positions[:, None]
        )
        scores = jnp.where(allowed[None], scores, -jnp.inf)
        highest = jnp.max(scores, axis=-1, keepdims=True)
        weights = jnp.exp(scores - highest)
        probs = (weights / jnp.sum(weights, axis=-1, keepdims=True)).astype(jnp.bfloat16)
        context = jnp.einsum("hqk,khd->qhd", probs, values, preferred_element_type=jnp.float32)
        return context.astype(jnp.bfloat16)

    starts = jnp.arange(total_tokens // span, dtype=jnp.int32) * span
    context = lax.map(one_block, starts).reshape(total_tokens, inner)
    return (context, keys.reshape(total_tokens, inner), values.reshape(total_tokens, inner))


def expert_apply(picked, gate_w, up_w, down_w):
    gate_part = jnp.dot(picked, gate_w, preferred_element_type=jnp.float32)
    upward = jnp.dot(picked, up_w, preferred_element_type=jnp.float32)
    hidden = (jax.nn.silu(gate_part) * upward).astype(jnp.bfloat16)
    return jnp.dot(hidden, down_w, preferred_element_type=jnp.float32).astype(jnp.bfloat16)


def ring_reduce_scatter(partial, groups):
    ring = groups // 4
    rows = partial.shape[0] // groups
    width = partial.shape[1]
    me = lax.axis_index("tensor")
    y = me // 4
    side = (me // 2) % 2
    core = me % 2
    blocks = partial.reshape(ring, 2, 2, rows, width)
    core_pairs = [(t, t ^ 1) for t in range(groups)]
    keep = lax.dynamic_index_in_dim(blocks, core, axis=2, keepdims=False)
    give = lax.dynamic_index_in_dim(blocks, 1 - core, axis=2, keepdims=False)
    got = lax.ppermute(give, "tensor", core_pairs)
    summed = keep.astype(jnp.float32) + got.astype(jnp.float32)
    half = width // 2
    forward_part = summed[..., :half]
    backward_part = summed[..., half:]
    forward_pairs = [(t, ((t // 4 + 1) % ring) * 4 + t % 4) for t in range(groups)]
    backward_pairs = [(t, ((t // 4 + ring - 1) % ring) * 4 + t % 4) for t in range(groups)]
    carry_f = lax.dynamic_index_in_dim(forward_part, (y + ring - 1) % ring, 0, False)
    carry_b = lax.dynamic_index_in_dim(backward_part, (y + 1) % ring, 0, False)
    carry_f = carry_f.astype(jnp.bfloat16)
    carry_b = carry_b.astype(jnp.bfloat16)
    for step in range(ring - 1):
        recv_f = lax.ppermute(carry_f, "tensor", forward_pairs)
        recv_b = lax.ppermute(carry_b, "tensor", backward_pairs)
        index_f = (y + 2 * ring - step - 2) % ring
        index_b = (y + step + 2) % ring
        acc_f = recv_f.astype(jnp.float32) + lax.dynamic_index_in_dim(
            forward_part, index_f, 0, False
        )
        acc_b = recv_b.astype(jnp.float32) + lax.dynamic_index_in_dim(
            backward_part, index_b, 0, False
        )
        carry_f = acc_f.astype(jnp.bfloat16)
        carry_b = acc_b.astype(jnp.bfloat16)
    mine = jnp.concatenate([acc_f, acc_b], axis=-1)
    side_pairs = [(t, t ^ 2) for t in range(groups)]
    keep_side = lax.dynamic_index_in_dim(mine, side, 0, False)
    give_side = lax.dynamic_index_in_dim(mine, 1 - side, 0, False).astype(jnp.bfloat16)
    got_side = lax.ppermute(give_side, "tensor", side_pairs)
    return keep_side + got_side.astype(jnp.float32)


def shards(
    tokens,
    segment_ids,
    attention_gain,
    query_weight,
    key_weight,
    value_weight,
    output_weight,
    ffn_gain,
    shared_gate,
    shared_up,
    shared_down,
    expert_gate,
    expert_up,
    expert_down,
    expert_ids,
    gate_weights,
    page_table,
):
    tok_dev = tokens.shape[0]
    groups = lax.axis_size("tensor")
    position = lax.axis_index("tensor")
    inner = query_weight.shape[1]
    head_count = inner // HD
    model_width = tokens.shape[1]

    projection = jnp.concatenate([query_weight, key_weight, value_weight], axis=1)
    normed_all = lax.all_gather(rms_scale(tokens, attention_gain), "tensor", axis=0, tiled=True)
    out_weight_all = lax.all_gather(output_weight, "tensor", axis=0, tiled=True)
    projected = jnp.dot(normed_all, projection, preferred_element_type=jnp.float32).astype(
        jnp.bfloat16
    )
    context, keys, values = attend(projected, segment_ids, head_count)
    cache = jnp.stack([keys, values]).reshape(2, -1, PAGE, inner)
    kv_pages = jnp.zeros_like(cache).at[:, page_table].set(cache)

    received = lax.all_to_all(
        context.reshape(groups, tok_dev, inner), "tensor", split_axis=0, concat_axis=0, tiled=True
    )
    partials = jnp.einsum(
        "gtd,gdo->gto",
        received,
        out_weight_all.reshape(groups, inner, model_width),
        preferred_element_type=jnp.float32,
    ).astype(jnp.bfloat16)
    attention = jnp.sum(partials.astype(jnp.float32), axis=0)
    residual = (tokens.astype(jnp.float32) + attention).astype(jnp.bfloat16)
    normed_ffn = rms_scale(residual, ffn_gain)
    pieces = 2
    piece_width = model_width // pieces
    stream_pieces = [
        lax.all_gather(
            normed_ffn[:, k * piece_width : (k + 1) * piece_width], "tensor", axis=0, tiled=True
        )
        for k in range(pieces)
    ]

    local_experts = expert_gate.shape[0]
    expert_count = local_experts * groups
    capacity = tok_dev * TOP // expert_count + tok_dev // 8
    id_blocks = expert_ids.reshape(groups, tok_dev, -1)
    gate_blocks = gate_weights.reshape(groups, tok_dev, -1)
    slots = jnp.arange(capacity, dtype=jnp.int32)
    onehots = []
    weights = []
    for local in range(local_experts):
        expert = position * local_experts + local
        chosen = id_blocks == expert
        hits = jnp.sum(chosen.astype(jnp.int32), axis=2)
        weights.append(jnp.sum(jnp.where(chosen, gate_blocks, 0.0), axis=2))
        rank = jnp.cumsum(hits, axis=1) - hits
        onehots.append(
            ((hits[:, None, :] > 0) & (rank[:, None, :] == slots[None, :, None])).astype(
                jnp.bfloat16
            )
        )

    shared_columns = jnp.concatenate([shared_gate, shared_up], axis=1)
    shared_width = shared_gate.shape[1]
    joined = None
    expert_gate_parts = [None] * local_experts
    expert_up_parts = [None] * local_experts
    for k in range(pieces):
        columns = slice(k * piece_width, (k + 1) * piece_width)
        piece = stream_pieces[k]
        step = jnp.dot(piece, shared_columns[columns], preferred_element_type=jnp.float32)
        joined = step if joined is None else joined + step
        token_blocks = piece.reshape(groups, tok_dev, piece_width)
        for local in range(local_experts):
            picked = jnp.einsum(
                "bst,btd->bsd", onehots[local], token_blocks, preferred_element_type=jnp.float32
            ).astype(jnp.bfloat16).reshape(-1, piece_width)
            g = jnp.dot(picked, expert_gate[local][columns], preferred_element_type=jnp.float32)
            u = jnp.dot(picked, expert_up[local][columns], preferred_element_type=jnp.float32)
            if expert_gate_parts[local] is None:
                expert_gate_parts[local], expert_up_parts[local] = g, u
            else:
                expert_gate_parts[local] = expert_gate_parts[local] + g
                expert_up_parts[local] = expert_up_parts[local] + u
    hidden_all = (jax.nn.silu(joined[:, :shared_width]) * joined[:, shared_width:]).astype(
        jnp.bfloat16
    )
    expert_hidden = [
        (jax.nn.silu(expert_gate_parts[local]) * expert_up_parts[local]).astype(jnp.bfloat16)
        for local in range(local_experts)
    ]

    outs = []
    for k in range(pieces):
        columns = slice(k * piece_width, (k + 1) * piece_width)
        term = jnp.dot(hidden_all, shared_down[:, columns], preferred_element_type=jnp.float32)
        for local in range(local_experts):
            rows = jnp.dot(
                expert_hidden[local], expert_down[local][:, columns], preferred_element_type=jnp.float32
            ).astype(jnp.bfloat16)
            back = jnp.einsum(
                "bst,bsd->btd",
                onehots[local],
                rows.reshape(groups, capacity, piece_width),
                preferred_element_type=jnp.float32,
            ).astype(jnp.bfloat16)
            term = term + weights[local].reshape(-1, 1) * back.reshape(-1, piece_width).astype(
                jnp.float32
            )
        outs.append(ring_reduce_scatter(term.astype(jnp.bfloat16), groups))
    ffn_out = jnp.concatenate(outs, axis=1)
    layer_out = (residual.astype(jnp.float32) + ffn_out).astype(jnp.bfloat16)
    return (layer_out, kv_pages)


def solution(mesh):
    placed = (
        P(("dp", "tensor"), None),
        P("dp"),
        P(),
        P(None, "tensor"),
        P(None, "tensor"),
        P(None, "tensor"),
        P("tensor", None),
        P(),
        P(None, "tensor"),
        P(None, "tensor"),
        P("tensor", None),
        P("tensor", None, None),
        P("tensor", None, None),
        P("tensor", None, None),
        P("dp", None),
        P("dp", None),
        P("dp"),
    )
    return jax.shard_map(
        shards,
        mesh=mesh,
        in_specs=placed,
        out_specs=(P(("dp", "tensor"), None), P(None, "dp", None, "tensor")),
        check_vma=False,
    )
```

```python
import jax
import jax.numpy as jnp
from jax import lax
from jax.sharding import PartitionSpec as P

HD = 128
TOP = 6
PAGE = 128


def rms_scale(hidden, gain):
    widened = hidden.astype(jnp.float32)
    inverse = lax.rsqrt(jnp.mean(widened * widened, axis=-1, keepdims=True) + 1e-06)
    return (widened * inverse * gain).astype(jnp.bfloat16)


def attend(projected, segment_ids, head_count):
    total_tokens = projected.shape[0]
    inner = head_count * HD
    queries = projected[:, :inner].reshape(total_tokens, head_count, HD)
    keys = projected[:, inner : 2 * inner].reshape(total_tokens, head_count, HD)
    values = projected[:, 2 * inner :].reshape(total_tokens, head_count, HD)
    scale = HD ** (-0.5)
    positions = jnp.arange(total_tokens, dtype=jnp.int32)
    span = min(512, total_tokens)

    def one_block(start):
        query_rows = lax.dynamic_slice_in_dim(queries, start, span, 0)
        query_segments = lax.dynamic_slice_in_dim(segment_ids, start, span, 0)
        query_positions = start + jnp.arange(span, dtype=jnp.int32)
        scores = (
            jnp.einsum("qhd,khd->hqk", query_rows, keys, preferred_element_type=jnp.float32) * scale
        )
        allowed = (query_segments[:, None] == segment_ids[None, :]) & (
            positions[None, :] <= query_positions[:, None]
        )
        scores = jnp.where(allowed[None], scores, -jnp.inf)
        highest = jnp.max(scores, axis=-1, keepdims=True)
        weights = jnp.exp(scores - highest)
        probs = (weights / jnp.sum(weights, axis=-1, keepdims=True)).astype(jnp.bfloat16)
        context = jnp.einsum("hqk,khd->qhd", probs, values, preferred_element_type=jnp.float32)
        return context.astype(jnp.bfloat16)

    starts = jnp.arange(total_tokens // span, dtype=jnp.int32) * span
    context = lax.map(one_block, starts).reshape(total_tokens, inner)
    return (context, keys.reshape(total_tokens, inner), values.reshape(total_tokens, inner))


def expert_apply(picked, gate_w, up_w, down_w):
    gate_part = jnp.dot(picked, gate_w, preferred_element_type=jnp.float32)
    upward = jnp.dot(picked, up_w, preferred_element_type=jnp.float32)
    hidden = (jax.nn.silu(gate_part) * upward).astype(jnp.bfloat16)
    return jnp.dot(hidden, down_w, preferred_element_type=jnp.float32).astype(jnp.bfloat16)


def ring_reduce_scatter(partial, groups):
    ring = groups // 4
    rows = partial.shape[0] // groups
    width = partial.shape[1]
    me = lax.axis_index("tensor")
    y = me // 4
    side = (me // 2) % 2
    core = me % 2
    blocks = partial.reshape(ring, 2, 2, rows, width)
    core_pairs = [(t, t ^ 1) for t in range(groups)]
    keep = lax.dynamic_index_in_dim(blocks, core, axis=2, keepdims=False)
    give = lax.dynamic_index_in_dim(blocks, 1 - core, axis=2, keepdims=False)
    got = lax.ppermute(give, "tensor", core_pairs)
    summed = keep.astype(jnp.float32) + got.astype(jnp.float32)
    half = width // 2
    forward_part = summed[..., :half]
    backward_part = summed[..., half:]
    forward_pairs = [(t, ((t // 4 + 1) % ring) * 4 + t % 4) for t in range(groups)]
    backward_pairs = [(t, ((t // 4 + ring - 1) % ring) * 4 + t % 4) for t in range(groups)]
    carry_f = lax.dynamic_index_in_dim(forward_part, (y + ring - 1) % ring, 0, False)
    carry_b = lax.dynamic_index_in_dim(backward_part, (y + 1) % ring, 0, False)
    carry_f = carry_f.astype(jnp.bfloat16)
    carry_b = carry_b.astype(jnp.bfloat16)
    for step in range(ring - 1):
        recv_f = lax.ppermute(carry_f, "tensor", forward_pairs)
        recv_b = lax.ppermute(carry_b, "tensor", backward_pairs)
        index_f = (y + 2 * ring - step - 2) % ring
        index_b = (y + step + 2) % ring
        acc_f = recv_f.astype(jnp.float32) + lax.dynamic_index_in_dim(
            forward_part, index_f, 0, False
        )
        acc_b = recv_b.astype(jnp.float32) + lax.dynamic_index_in_dim(
            backward_part, index_b, 0, False
        )
        carry_f = acc_f.astype(jnp.bfloat16)
        carry_b = acc_b.astype(jnp.bfloat16)
    mine = jnp.concatenate([acc_f, acc_b], axis=-1)
    side_pairs = [(t, t ^ 2) for t in range(groups)]
    keep_side = lax.dynamic_index_in_dim(mine, side, 0, False)
    give_side = lax.dynamic_index_in_dim(mine, 1 - side, 0, False).astype(jnp.bfloat16)
    got_side = lax.ppermute(give_side, "tensor", side_pairs)
    return keep_side + got_side.astype(jnp.float32)


def shards(
    tokens,
    segment_ids,
    attention_gain,
    query_weight,
    key_weight,
    value_weight,
    output_weight,
    ffn_gain,
    shared_gate,
    shared_up,
    shared_down,
    expert_gate,
    expert_up,
    expert_down,
    expert_ids,
    gate_weights,
    page_table,
):
    tok_dev = tokens.shape[0]
    groups = lax.axis_size("tensor")
    position = lax.axis_index("tensor")
    inner = query_weight.shape[1]
    head_count = inner // HD
    model_width = tokens.shape[1]

    projection = jnp.concatenate([query_weight, key_weight, value_weight], axis=1)
    normed_all = lax.all_gather(rms_scale(tokens, attention_gain), "tensor", axis=0, tiled=True)
    out_weight_all = lax.all_gather(output_weight, "tensor", axis=0, tiled=True)
    projected = jnp.dot(normed_all, projection, preferred_element_type=jnp.float32).astype(
        jnp.bfloat16
    )
    context, keys, values = attend(projected, segment_ids, head_count)
    cache = jnp.stack([keys, values]).reshape(2, -1, PAGE, inner)
    kv_pages = jnp.zeros_like(cache).at[:, page_table].set(cache)

    received = lax.all_to_all(
        context.reshape(groups, tok_dev, inner), "tensor", split_axis=0, concat_axis=0, tiled=True
    )
    partials = jnp.einsum(
        "gtd,gdo->gto",
        received,
        out_weight_all.reshape(groups, inner, model_width),
        preferred_element_type=jnp.float32,
    ).astype(jnp.bfloat16)
    attention = jnp.sum(partials.astype(jnp.float32), axis=0)
    residual = (tokens.astype(jnp.float32) + attention).astype(jnp.bfloat16)
    normed_ffn = rms_scale(residual, ffn_gain)
    pieces = 2
    piece_width = model_width // pieces
    normed_stream = lax.all_gather(normed_ffn, "tensor", axis=0, tiled=True)

    local_experts = expert_gate.shape[0]
    expert_count = local_experts * groups
    capacity = tok_dev * TOP // expert_count + tok_dev // 8
    id_blocks = expert_ids.reshape(groups, tok_dev, -1)
    gate_blocks = gate_weights.reshape(groups, tok_dev, -1)
    slots = jnp.arange(capacity, dtype=jnp.int32)
    onehots = []
    weights = []
    for local in range(local_experts):
        expert = position * local_experts + local
        chosen = id_blocks == expert
        hits = jnp.sum(chosen.astype(jnp.int32), axis=2)
        weights.append(jnp.sum(jnp.where(chosen, gate_blocks, 0.0), axis=2))
        rank = jnp.cumsum(hits, axis=1) - hits
        onehots.append(
            ((hits[:, None, :] > 0) & (rank[:, None, :] == slots[None, :, None])).astype(
                jnp.bfloat16
            )
        )

    shared_columns = jnp.concatenate([shared_gate, shared_up], axis=1)
    shared_width = shared_gate.shape[1]
    joined = jnp.dot(normed_stream, shared_columns, preferred_element_type=jnp.float32)
    token_blocks = normed_stream.reshape(groups, tok_dev, model_width)
    expert_gate_parts = []
    expert_up_parts = []
    for local in range(local_experts):
        picked = jnp.einsum(
            "bst,btd->bsd", onehots[local], token_blocks, preferred_element_type=jnp.float32
        ).astype(jnp.bfloat16).reshape(-1, model_width)
        expert_gate_parts.append(
            jnp.dot(picked, expert_gate[local], preferred_element_type=jnp.float32)
        )
        expert_up_parts.append(jnp.dot(picked, expert_up[local], preferred_element_type=jnp.float32))
    hidden_all = (jax.nn.silu(joined[:, :shared_width]) * joined[:, shared_width:]).astype(
        jnp.bfloat16
    )
    expert_hidden = [
        (jax.nn.silu(expert_gate_parts[local]) * expert_up_parts[local]).astype(jnp.bfloat16)
        for local in range(local_experts)
    ]

    outs = []
    for k in range(pieces):
        columns = slice(k * piece_width, (k + 1) * piece_width)
        term = jnp.dot(hidden_all, shared_down[:, columns], preferred_element_type=jnp.float32)
        for local in range(local_experts):
            rows = jnp.dot(
                expert_hidden[local], expert_down[local][:, columns], preferred_element_type=jnp.float32
            ).astype(jnp.bfloat16)
            back = jnp.einsum(
                "bst,bsd->btd",
                onehots[local],
                rows.reshape(groups, capacity, piece_width),
                preferred_element_type=jnp.float32,
            ).astype(jnp.bfloat16)
            term = term + weights[local].reshape(-1, 1) * back.reshape(-1, piece_width).astype(
                jnp.float32
            )
        outs.append(ring_reduce_scatter(term.astype(jnp.bfloat16), groups))
    ffn_out = jnp.concatenate(outs, axis=1)
    layer_out = (residual.astype(jnp.float32) + ffn_out).astype(jnp.bfloat16)
    return (layer_out, kv_pages)


def solution(mesh):
    placed = (
        P(("dp", "tensor"), None),
        P("dp"),
        P(),
        P(None, "tensor"),
        P(None, "tensor"),
        P(None, "tensor"),
        P("tensor", None),
        P(),
        P(None, "tensor"),
        P(None, "tensor"),
        P("tensor", None),
        P("tensor", None, None),
        P("tensor", None, None),
        P("tensor", None, None),
        P("dp", None),
        P("dp", None),
        P("dp"),
    )
    return jax.shard_map(
        shards,
        mesh=mesh,
        in_specs=placed,
        out_specs=(P(("dp", "tensor"), None), P(None, "dp", None, "tensor")),
        check_vma=False,
    )
```

```python
import jax
import jax.numpy as jnp
from jax import lax
from jax.sharding import PartitionSpec as P

HD = 128
TOP = 6
PAGE = 128


def rms_scale(hidden, gain):
    widened = hidden.astype(jnp.float32)
    inverse = lax.rsqrt(jnp.mean(widened * widened, axis=-1, keepdims=True) + 1e-06)
    return (widened * inverse * gain).astype(jnp.bfloat16)


def attend(projected, segment_ids, head_count):
    total_tokens = projected.shape[0]
    inner = head_count * HD
    queries = projected[:, :inner].reshape(total_tokens, head_count, HD)
    keys = projected[:, inner : 2 * inner].reshape(total_tokens, head_count, HD)
    values = projected[:, 2 * inner :].reshape(total_tokens, head_count, HD)
    scale = HD ** (-0.5)
    positions = jnp.arange(total_tokens, dtype=jnp.int32)
    span = min(512, total_tokens)

    def one_block(start):
        query_rows = lax.dynamic_slice_in_dim(queries, start, span, 0)
        query_segments = lax.dynamic_slice_in_dim(segment_ids, start, span, 0)
        query_positions = start + jnp.arange(span, dtype=jnp.int32)
        scores = (
            jnp.einsum("qhd,khd->hqk", query_rows, keys, preferred_element_type=jnp.float32) * scale
        )
        allowed = (query_segments[:, None] == segment_ids[None, :]) & (
            positions[None, :] <= query_positions[:, None]
        )
        scores = jnp.where(allowed[None], scores, -jnp.inf)
        highest = jnp.max(scores, axis=-1, keepdims=True)
        weights = jnp.exp(scores - highest)
        probs = (weights / jnp.sum(weights, axis=-1, keepdims=True)).astype(jnp.bfloat16)
        context = jnp.einsum("hqk,khd->qhd", probs, values, preferred_element_type=jnp.float32)
        return context.astype(jnp.bfloat16)

    starts = jnp.arange(total_tokens // span, dtype=jnp.int32) * span
    context = lax.map(one_block, starts).reshape(total_tokens, inner)
    return (context, keys.reshape(total_tokens, inner), values.reshape(total_tokens, inner))


def expert_apply(picked, gate_w, up_w, down_w):
    gate_part = jnp.dot(picked, gate_w, preferred_element_type=jnp.float32)
    upward = jnp.dot(picked, up_w, preferred_element_type=jnp.float32)
    hidden = (jax.nn.silu(gate_part) * upward).astype(jnp.bfloat16)
    return jnp.dot(hidden, down_w, preferred_element_type=jnp.float32).astype(jnp.bfloat16)


def ring_reduce_scatter(partial, groups):
    ring = groups // 4
    rows = partial.shape[0] // groups
    width = partial.shape[1]
    me = lax.axis_index("tensor")
    y = me // 4
    side = (me // 2) % 2
    core = me % 2
    blocks = partial.reshape(ring, 2, 2, rows, width)
    core_pairs = [(t, t ^ 1) for t in range(groups)]
    keep = lax.dynamic_index_in_dim(blocks, core, axis=2, keepdims=False)
    give = lax.dynamic_index_in_dim(blocks, 1 - core, axis=2, keepdims=False)
    got = lax.ppermute(give, "tensor", core_pairs)
    summed = keep.astype(jnp.float32) + got.astype(jnp.float32)
    half = width // 2
    forward_part = summed[..., :half]
    backward_part = summed[..., half:]
    forward_pairs = [(t, ((t // 4 + 1) % ring) * 4 + t % 4) for t in range(groups)]
    backward_pairs = [(t, ((t // 4 + ring - 1) % ring) * 4 + t % 4) for t in range(groups)]
    carry_f = lax.dynamic_index_in_dim(forward_part, (y + ring - 1) % ring, 0, False)
    carry_b = lax.dynamic_index_in_dim(backward_part, (y + 1) % ring, 0, False)
    carry_f = carry_f.astype(jnp.bfloat16)
    carry_b = carry_b.astype(jnp.bfloat16)
    for step in range(ring - 1):
        recv_f = lax.ppermute(carry_f, "tensor", forward_pairs)
        recv_b = lax.ppermute(carry_b, "tensor", backward_pairs)
        index_f = (y + 2 * ring - step - 2) % ring
        index_b = (y + step + 2) % ring
        acc_f = recv_f.astype(jnp.float32) + lax.dynamic_index_in_dim(
            forward_part, index_f, 0, False
        )
        acc_b = recv_b.astype(jnp.float32) + lax.dynamic_index_in_dim(
            backward_part, index_b, 0, False
        )
        carry_f = acc_f.astype(jnp.bfloat16)
        carry_b = acc_b.astype(jnp.bfloat16)
    mine = jnp.concatenate([acc_f, acc_b], axis=-1)
    side_pairs = [(t, t ^ 2) for t in range(groups)]
    keep_side = lax.dynamic_index_in_dim(mine, side, 0, False)
    give_side = lax.dynamic_index_in_dim(mine, 1 - side, 0, False).astype(jnp.bfloat16)
    got_side = lax.ppermute(give_side, "tensor", side_pairs)
    return keep_side + got_side.astype(jnp.float32)


def weight_gather(block, groups):
    ring = groups // 4
    me = lax.axis_index("tensor")
    y = me // 4
    side = (me // 2) % 2
    core = me % 2
    side_pairs = [(t, t ^ 2) for t in range(groups)]
    core_pairs = [(t, t ^ 1) for t in range(groups)]
    forward_pairs = [(t, ((t // 4 + 1) % ring) * 4 + t % 4) for t in range(groups)]
    backward_pairs = [(t, ((t // 4 + ring - 1) % ring) * 4 + t % 4) for t in range(groups)]
    other_side = lax.ppermute(block, "tensor", side_pairs)
    pair = jnp.stack([block, other_side])
    from_prev = lax.ppermute(pair, "tensor", forward_pairs)
    from_next = lax.ppermute(pair, "tensor", backward_pairs)
    half = block.shape[1] // 2
    far_a = lax.ppermute(from_prev[..., :half], "tensor", forward_pairs)
    far_b = lax.ppermute(from_next[..., half:], "tensor", backward_pairs)
    far = jnp.concatenate([far_a, far_b], axis=-1)
    mine = jnp.stack([pair, from_next, far, from_prev])
    other_core = lax.ppermute(mine, "tensor", core_pairs)
    offsets = jnp.array([0, 1, 2, ring - 1], jnp.int32)
    rows_y = (y + offsets) % ring
    sides = jnp.stack([side, 1 - side])
    owner_mine = (rows_y[:, None] * 2 + sides[None, :]) * 2 + core
    owner_other = owner_mine - core + (1 - core)
    return (mine, other_core), (owner_mine, owner_other)


def shards(
    tokens,
    segment_ids,
    attention_gain,
    query_weight,
    key_weight,
    value_weight,
    output_weight,
    ffn_gain,
    shared_gate,
    shared_up,
    shared_down,
    expert_gate,
    expert_up,
    expert_down,
    expert_ids,
    gate_weights,
    page_table,
):
    tok_dev = tokens.shape[0]
    groups = lax.axis_size("tensor")
    position = lax.axis_index("tensor")
    inner = query_weight.shape[1]
    head_count = inner // HD
    model_width = tokens.shape[1]

    projection = jnp.concatenate([query_weight, key_weight, value_weight], axis=1)
    normed_all = lax.all_gather(rms_scale(tokens, attention_gain), "tensor", axis=0, tiled=True)
    weight_pieces, piece_owners = weight_gather(output_weight, groups)
    projected = jnp.dot(normed_all, projection, preferred_element_type=jnp.float32).astype(
        jnp.bfloat16
    )
    context, keys, values = attend(projected, segment_ids, head_count)
    cache = jnp.stack([keys, values]).reshape(2, -1, PAGE, inner)
    kv_pages = jnp.zeros_like(cache).at[:, page_table].set(cache)

    received = lax.all_to_all(
        context.reshape(groups, tok_dev, inner), "tensor", split_axis=0, concat_axis=0, tiled=True
    )
    attention = jnp.zeros((tok_dev, model_width), jnp.float32)
    for weight_piece, owner in zip(weight_pieces, piece_owners):
        context_piece = jnp.take(received, owner.reshape(-1), axis=0)
        partials = jnp.einsum(
            "gtd,gdo->gto",
            context_piece,
            weight_piece.reshape(-1, inner, model_width),
            preferred_element_type=jnp.float32,
        ).astype(jnp.bfloat16)
        attention = attention + jnp.sum(partials.astype(jnp.float32), axis=0)
    residual = (tokens.astype(jnp.float32) + attention).astype(jnp.bfloat16)
    normed_ffn = rms_scale(residual, ffn_gain)
    pieces = 2
    piece_width = model_width // pieces
    normed_stream = lax.all_gather(normed_ffn, "tensor", axis=0, tiled=True)

    local_experts = expert_gate.shape[0]
    expert_count = local_experts * groups
    capacity = tok_dev * TOP // expert_count + tok_dev // 8
    id_blocks = expert_ids.reshape(groups, tok_dev, -1)
    gate_blocks = gate_weights.reshape(groups, tok_dev, -1)
    slots = jnp.arange(capacity, dtype=jnp.int32)
    onehots = []
    weights = []
    for local in range(local_experts):
        expert = position * local_experts + local
        chosen = id_blocks == expert
        hits = jnp.sum(chosen.astype(jnp.int32), axis=2)
        weights.append(jnp.sum(jnp.where(chosen, gate_blocks, 0.0), axis=2))
        rank = jnp.cumsum(hits, axis=1) - hits
        onehots.append(
            ((hits[:, None, :] > 0) & (rank[:, None, :] == slots[None, :, None])).astype(
                jnp.bfloat16
            )
        )

    shared_columns = jnp.concatenate([shared_gate, shared_up], axis=1)
    shared_width = shared_gate.shape[1]
    joined = jnp.dot(normed_stream, shared_columns, preferred_element_type=jnp.float32)
    token_blocks = normed_stream.reshape(groups, tok_dev, model_width)
    expert_gate_parts = []
    expert_up_parts = []
    for local in range(local_experts):
        picked = jnp.einsum(
            "bst,btd->bsd", onehots[local], token_blocks, preferred_element_type=jnp.float32
        ).astype(jnp.bfloat16).reshape(-1, model_width)
        expert_gate_parts.append(
            jnp.dot(picked, expert_gate[local], preferred_element_type=jnp.float32)
        )
        expert_up_parts.append(jnp.dot(picked, expert_up[local], preferred_element_type=jnp.float32))
    hidden_all = (jax.nn.silu(joined[:, :shared_width]) * joined[:, shared_width:]).astype(
        jnp.bfloat16
    )
    expert_hidden = [
        (jax.nn.silu(expert_gate_parts[local]) * expert_up_parts[local]).astype(jnp.bfloat16)
        for local in range(local_experts)
    ]

    outs = []
    for k in range(pieces):
        columns = slice(k * piece_width, (k + 1) * piece_width)
        term = jnp.dot(hidden_all, shared_down[:, columns], preferred_element_type=jnp.float32)
        for local in range(local_experts):
            rows = jnp.dot(
                expert_hidden[local], expert_down[local][:, columns], preferred_element_type=jnp.float32
            ).astype(jnp.bfloat16)
            back = jnp.einsum(
                "bst,bsd->btd",
                onehots[local],
                rows.reshape(groups, capacity, piece_width),
                preferred_element_type=jnp.float32,
            ).astype(jnp.bfloat16)
            term = term + weights[local].reshape(-1, 1) * back.reshape(-1, piece_width).astype(
                jnp.float32
            )
        outs.append(ring_reduce_scatter(term.astype(jnp.bfloat16), groups))
    ffn_out = jnp.concatenate(outs, axis=1)
    layer_out = (residual.astype(jnp.float32) + ffn_out).astype(jnp.bfloat16)
    return (layer_out, kv_pages)


def solution(mesh):
    placed = (
        P(("dp", "tensor"), None),
        P("dp"),
        P(),
        P(None, "tensor"),
        P(None, "tensor"),
        P(None, "tensor"),
        P("tensor", None),
        P(),
        P(None, "tensor"),
        P(None, "tensor"),
        P("tensor", None),
        P("tensor", None, None),
        P("tensor", None, None),
        P("tensor", None, None),
        P("dp", None),
        P("dp", None),
        P("dp"),
    )
    return jax.shard_map(
        shards,
        mesh=mesh,
        in_specs=placed,
        out_specs=(P(("dp", "tensor"), None), P(None, "dp", None, "tensor")),
        check_vma=False,
    )
```

```python
import jax
import jax.numpy as jnp
from jax import lax
from jax.sharding import PartitionSpec as P

HD = 128
TOP = 6
PAGE = 128


def rms_scale(hidden, gain):
    widened = hidden.astype(jnp.float32)
    inverse = lax.rsqrt(jnp.mean(widened * widened, axis=-1, keepdims=True) + 1e-06)
    return (widened * inverse * gain).astype(jnp.bfloat16)


def attend(projected, segment_ids, head_count):
    total_tokens = projected.shape[0]
    inner = head_count * HD
    queries = projected[:, :inner].reshape(total_tokens, head_count, HD)
    keys = projected[:, inner : 2 * inner].reshape(total_tokens, head_count, HD)
    values = projected[:, 2 * inner :].reshape(total_tokens, head_count, HD)
    scale = HD ** (-0.5)
    positions = jnp.arange(total_tokens, dtype=jnp.int32)
    span = min(512, total_tokens)

    def one_block(start):
        query_rows = lax.dynamic_slice_in_dim(queries, start, span, 0)
        query_segments = lax.dynamic_slice_in_dim(segment_ids, start, span, 0)
        query_positions = start + jnp.arange(span, dtype=jnp.int32)
        scores = (
            jnp.einsum("qhd,khd->hqk", query_rows, keys, preferred_element_type=jnp.float32) * scale
        )
        allowed = (query_segments[:, None] == segment_ids[None, :]) & (
            positions[None, :] <= query_positions[:, None]
        )
        scores = jnp.where(allowed[None], scores, -jnp.inf)
        highest = jnp.max(scores, axis=-1, keepdims=True)
        weights = jnp.exp(scores - highest)
        probs = (weights / jnp.sum(weights, axis=-1, keepdims=True)).astype(jnp.bfloat16)
        context = jnp.einsum("hqk,khd->qhd", probs, values, preferred_element_type=jnp.float32)
        return context.astype(jnp.bfloat16)

    starts = jnp.arange(total_tokens // span, dtype=jnp.int32) * span
    context = lax.map(one_block, starts).reshape(total_tokens, inner)
    return (context, keys.reshape(total_tokens, inner), values.reshape(total_tokens, inner))


def expert_apply(picked, gate_w, up_w, down_w):
    gate_part = jnp.dot(picked, gate_w, preferred_element_type=jnp.float32)
    upward = jnp.dot(picked, up_w, preferred_element_type=jnp.float32)
    hidden = (jax.nn.silu(gate_part) * upward).astype(jnp.bfloat16)
    return jnp.dot(hidden, down_w, preferred_element_type=jnp.float32).astype(jnp.bfloat16)


def ring_reduce_scatter(partial, groups):
    ring = groups // 4
    rows = partial.shape[0] // groups
    width = partial.shape[1]
    me = lax.axis_index("tensor")
    y = me // 4
    side = (me // 2) % 2
    core = me % 2
    blocks = partial.reshape(ring, 2, 2, rows, width)
    core_pairs = [(t, t ^ 1) for t in range(groups)]
    keep = lax.dynamic_index_in_dim(blocks, core, axis=2, keepdims=False)
    give = lax.dynamic_index_in_dim(blocks, 1 - core, axis=2, keepdims=False)
    got = lax.ppermute(give, "tensor", core_pairs)
    summed = keep.astype(jnp.float32) + got.astype(jnp.float32)
    half = width // 2
    forward_part = summed[..., :half]
    backward_part = summed[..., half:]
    forward_pairs = [(t, ((t // 4 + 1) % ring) * 4 + t % 4) for t in range(groups)]
    backward_pairs = [(t, ((t // 4 + ring - 1) % ring) * 4 + t % 4) for t in range(groups)]
    carry_f = lax.dynamic_index_in_dim(forward_part, (y + ring - 1) % ring, 0, False)
    carry_b = lax.dynamic_index_in_dim(backward_part, (y + 1) % ring, 0, False)
    carry_f = carry_f.astype(jnp.bfloat16)
    carry_b = carry_b.astype(jnp.bfloat16)
    for step in range(ring - 1):
        recv_f = lax.ppermute(carry_f, "tensor", forward_pairs)
        recv_b = lax.ppermute(carry_b, "tensor", backward_pairs)
        index_f = (y + 2 * ring - step - 2) % ring
        index_b = (y + step + 2) % ring
        acc_f = recv_f.astype(jnp.float32) + lax.dynamic_index_in_dim(
            forward_part, index_f, 0, False
        )
        acc_b = recv_b.astype(jnp.float32) + lax.dynamic_index_in_dim(
            backward_part, index_b, 0, False
        )
        carry_f = acc_f.astype(jnp.bfloat16)
        carry_b = acc_b.astype(jnp.bfloat16)
    mine = jnp.concatenate([acc_f, acc_b], axis=-1)
    side_pairs = [(t, t ^ 2) for t in range(groups)]
    keep_side = lax.dynamic_index_in_dim(mine, side, 0, False)
    give_side = lax.dynamic_index_in_dim(mine, 1 - side, 0, False).astype(jnp.bfloat16)
    got_side = lax.ppermute(give_side, "tensor", side_pairs)
    return keep_side + got_side.astype(jnp.float32)


def shards(
    tokens,
    segment_ids,
    attention_gain,
    query_weight,
    key_weight,
    value_weight,
    output_weight,
    ffn_gain,
    shared_gate,
    shared_up,
    shared_down,
    expert_gate,
    expert_up,
    expert_down,
    expert_ids,
    gate_weights,
    page_table,
):
    tok_dev = tokens.shape[0]
    groups = lax.axis_size("tensor")
    position = lax.axis_index("tensor")
    inner = query_weight.shape[1]
    head_count = inner // HD
    model_width = tokens.shape[1]

    projection = jnp.concatenate([query_weight, key_weight, value_weight], axis=1)
    normed_all = lax.all_gather(rms_scale(tokens, attention_gain), "tensor", axis=0, tiled=True)
    out_weight_all = lax.all_gather(output_weight, "tensor", axis=0, tiled=True)
    projected = jnp.dot(normed_all, projection, preferred_element_type=jnp.float32).astype(
        jnp.bfloat16
    )
    context, keys, values = attend(projected, segment_ids, head_count)
    cache = jnp.stack([keys, values]).reshape(2, -1, PAGE, inner)
    kv_pages = jnp.zeros_like(cache).at[:, page_table].set(cache)

    received = lax.all_to_all(
        context.reshape(groups, tok_dev, inner), "tensor", split_axis=0, concat_axis=0, tiled=True
    )
    context_rows = received.transpose(1, 0, 2).reshape(tok_dev, groups * inner)
    attention = jnp.dot(context_rows, out_weight_all, preferred_element_type=jnp.float32)
    residual = (tokens.astype(jnp.float32) + attention).astype(jnp.bfloat16)
    normed_ffn = rms_scale(residual, ffn_gain)
    pieces = 2
    piece_width = model_width // pieces
    normed_stream = lax.all_gather(normed_ffn, "tensor", axis=0, tiled=True)

    local_experts = expert_gate.shape[0]
    expert_count = local_experts * groups
    capacity = tok_dev * TOP // expert_count + tok_dev // 8
    id_blocks = expert_ids.reshape(groups, tok_dev, -1)
    gate_blocks = gate_weights.reshape(groups, tok_dev, -1)
    slots = jnp.arange(capacity, dtype=jnp.int32)
    onehots = []
    weights = []
    for local in range(local_experts):
        expert = position * local_experts + local
        chosen = id_blocks == expert
        hits = jnp.sum(chosen.astype(jnp.int32), axis=2)
        weights.append(jnp.sum(jnp.where(chosen, gate_blocks, 0.0), axis=2))
        rank = jnp.cumsum(hits, axis=1) - hits
        onehots.append(
            ((hits[:, None, :] > 0) & (rank[:, None, :] == slots[None, :, None])).astype(
                jnp.bfloat16
            )
        )

    shared_columns = jnp.concatenate([shared_gate, shared_up], axis=1)
    shared_width = shared_gate.shape[1]
    joined = jnp.dot(normed_stream, shared_columns, preferred_element_type=jnp.float32)
    token_blocks = normed_stream.reshape(groups, tok_dev, model_width)
    expert_gate_parts = []
    expert_up_parts = []
    for local in range(local_experts):
        picked = jnp.einsum(
            "bst,btd->bsd", onehots[local], token_blocks, preferred_element_type=jnp.float32
        ).astype(jnp.bfloat16).reshape(-1, model_width)
        expert_gate_parts.append(
            jnp.dot(picked, expert_gate[local], preferred_element_type=jnp.float32)
        )
        expert_up_parts.append(jnp.dot(picked, expert_up[local], preferred_element_type=jnp.float32))
    hidden_all = (jax.nn.silu(joined[:, :shared_width]) * joined[:, shared_width:]).astype(
        jnp.bfloat16
    )
    expert_hidden = [
        (jax.nn.silu(expert_gate_parts[local]) * expert_up_parts[local]).astype(jnp.bfloat16)
        for local in range(local_experts)
    ]

    outs = []
    for k in range(pieces):
        columns = slice(k * piece_width, (k + 1) * piece_width)
        term = jnp.dot(hidden_all, shared_down[:, columns], preferred_element_type=jnp.float32)
        for local in range(local_experts):
            rows = jnp.dot(
                expert_hidden[local], expert_down[local][:, columns], preferred_element_type=jnp.float32
            ).astype(jnp.bfloat16)
            back = jnp.einsum(
                "bst,bsd->btd",
                onehots[local],
                rows.reshape(groups, capacity, piece_width),
                preferred_element_type=jnp.float32,
            ).astype(jnp.bfloat16)
            term = term + weights[local].reshape(-1, 1) * back.reshape(-1, piece_width).astype(
                jnp.float32
            )
        outs.append(ring_reduce_scatter(term.astype(jnp.bfloat16), groups))
    ffn_out = jnp.concatenate(outs, axis=1)
    layer_out = (residual.astype(jnp.float32) + ffn_out).astype(jnp.bfloat16)
    return (layer_out, kv_pages)


def solution(mesh):
    placed = (
        P(("dp", "tensor"), None),
        P("dp"),
        P(),
        P(None, "tensor"),
        P(None, "tensor"),
        P(None, "tensor"),
        P("tensor", None),
        P(),
        P(None, "tensor"),
        P(None, "tensor"),
        P("tensor", None),
        P("tensor", None, None),
        P("tensor", None, None),
        P("tensor", None, None),
        P("dp", None),
        P("dp", None),
        P("dp"),
    )
    return jax.shard_map(
        shards,
        mesh=mesh,
        in_specs=placed,
        out_specs=(P(("dp", "tensor"), None), P(None, "dp", None, "tensor")),
        check_vma=False,
    )
```

```python
import jax
import jax.numpy as jnp
from jax import lax
from jax.sharding import PartitionSpec as P

HD = 128
TOP = 6
PAGE = 128


def rms_scale(hidden, gain):
    widened = hidden.astype(jnp.float32)
    inverse = lax.rsqrt(jnp.mean(widened * widened, axis=-1, keepdims=True) + 1e-06)
    return (widened * inverse * gain).astype(jnp.bfloat16)


def attend(projected, segment_ids, head_count):
    total_tokens = projected.shape[0]
    inner = head_count * HD
    queries = projected[:, :inner].reshape(total_tokens, head_count, HD)
    keys = projected[:, inner : 2 * inner].reshape(total_tokens, head_count, HD)
    values = projected[:, 2 * inner :].reshape(total_tokens, head_count, HD)
    scale = HD ** (-0.5)
    positions = jnp.arange(total_tokens, dtype=jnp.int32)
    span = min(512, total_tokens)

    def one_block(start):
        query_rows = lax.dynamic_slice_in_dim(queries, start, span, 0)
        query_segments = lax.dynamic_slice_in_dim(segment_ids, start, span, 0)
        query_positions = start + jnp.arange(span, dtype=jnp.int32)
        scores = (
            jnp.einsum("qhd,khd->hqk", query_rows, keys, preferred_element_type=jnp.float32) * scale
        )
        allowed = (query_segments[:, None] == segment_ids[None, :]) & (
            positions[None, :] <= query_positions[:, None]
        )
        scores = jnp.where(allowed[None], scores, -jnp.inf)
        highest = jnp.max(scores, axis=-1, keepdims=True)
        weights = jnp.exp(scores - highest)
        probs = (weights / jnp.sum(weights, axis=-1, keepdims=True)).astype(jnp.bfloat16)
        context = jnp.einsum("hqk,khd->qhd", probs, values, preferred_element_type=jnp.float32)
        return context.astype(jnp.bfloat16)

    starts = jnp.arange(total_tokens // span, dtype=jnp.int32) * span
    context = lax.map(one_block, starts).reshape(total_tokens, inner)
    return (context, keys.reshape(total_tokens, inner), values.reshape(total_tokens, inner))


def expert_apply(picked, gate_w, up_w, down_w):
    gate_part = jnp.dot(picked, gate_w, preferred_element_type=jnp.float32)
    upward = jnp.dot(picked, up_w, preferred_element_type=jnp.float32)
    hidden = (jax.nn.silu(gate_part) * upward).astype(jnp.bfloat16)
    return jnp.dot(hidden, down_w, preferred_element_type=jnp.float32).astype(jnp.bfloat16)


def ring_reduce_scatter(partial, groups):
    ring = groups // 4
    rows = partial.shape[0] // groups
    width = partial.shape[1]
    me = lax.axis_index("tensor")
    y = me // 4
    side = (me // 2) % 2
    core = me % 2
    blocks = partial.reshape(ring, 2, 2, rows, width)
    core_pairs = [(t, t ^ 1) for t in range(groups)]
    keep = lax.dynamic_index_in_dim(blocks, core, axis=2, keepdims=False)
    give = lax.dynamic_index_in_dim(blocks, 1 - core, axis=2, keepdims=False)
    got = lax.ppermute(give, "tensor", core_pairs)
    summed = keep.astype(jnp.float32) + got.astype(jnp.float32)
    half = width // 2
    forward_part = summed[..., :half]
    backward_part = summed[..., half:]
    forward_pairs = [(t, ((t // 4 + 1) % ring) * 4 + t % 4) for t in range(groups)]
    backward_pairs = [(t, ((t // 4 + ring - 1) % ring) * 4 + t % 4) for t in range(groups)]
    carry_f = lax.dynamic_index_in_dim(forward_part, (y + ring - 1) % ring, 0, False)
    carry_b = lax.dynamic_index_in_dim(backward_part, (y + 1) % ring, 0, False)
    carry_f = carry_f.astype(jnp.bfloat16)
    carry_b = carry_b.astype(jnp.bfloat16)
    for step in range(ring - 1):
        recv_f = lax.ppermute(carry_f, "tensor", forward_pairs)
        recv_b = lax.ppermute(carry_b, "tensor", backward_pairs)
        index_f = (y + 2 * ring - step - 2) % ring
        index_b = (y + step + 2) % ring
        acc_f = recv_f.astype(jnp.float32) + lax.dynamic_index_in_dim(
            forward_part, index_f, 0, False
        )
        acc_b = recv_b.astype(jnp.float32) + lax.dynamic_index_in_dim(
            backward_part, index_b, 0, False
        )
        carry_f = acc_f.astype(jnp.bfloat16)
        carry_b = acc_b.astype(jnp.bfloat16)
    mine = jnp.concatenate([acc_f, acc_b], axis=-1)
    side_pairs = [(t, t ^ 2) for t in range(groups)]
    keep_side = lax.dynamic_index_in_dim(mine, side, 0, False)
    give_side = lax.dynamic_index_in_dim(mine, 1 - side, 0, False).astype(jnp.bfloat16)
    got_side = lax.ppermute(give_side, "tensor", side_pairs)
    return keep_side + got_side.astype(jnp.float32)


def shards(
    tokens,
    segment_ids,
    attention_gain,
    query_weight,
    key_weight,
    value_weight,
    output_weight,
    ffn_gain,
    shared_gate,
    shared_up,
    shared_down,
    expert_gate,
    expert_up,
    expert_down,
    expert_ids,
    gate_weights,
    page_table,
):
    tok_dev = tokens.shape[0]
    groups = lax.axis_size("tensor")
    position = lax.axis_index("tensor")
    inner = query_weight.shape[1]
    head_count = inner // HD
    model_width = tokens.shape[1]

    projection = jnp.concatenate([query_weight, key_weight, value_weight], axis=1)
    normed_all = lax.all_gather(rms_scale(tokens, attention_gain), "tensor", axis=0, tiled=True)
    out_weight_all = lax.all_gather(output_weight, "tensor", axis=0, tiled=True)
    projected = lax.map(
        lambda rows: jnp.dot(rows, projection, preferred_element_type=jnp.float32).astype(
            jnp.bfloat16
        ),
        normed_all.reshape(4, -1, normed_all.shape[1]),
    ).reshape(normed_all.shape[0], -1)
    context, keys, values = attend(projected, segment_ids, head_count)
    cache = jnp.stack([keys, values]).reshape(2, -1, PAGE, inner)
    kv_pages = jnp.zeros_like(cache).at[:, page_table].set(cache)

    received = lax.all_to_all(
        context.reshape(groups, tok_dev, inner), "tensor", split_axis=0, concat_axis=0, tiled=True
    )
    context_rows = received.transpose(1, 0, 2).reshape(tok_dev, groups * inner)
    attention = jnp.dot(context_rows, out_weight_all, preferred_element_type=jnp.float32)
    residual = (tokens.astype(jnp.float32) + attention).astype(jnp.bfloat16)
    normed_ffn = rms_scale(residual, ffn_gain)
    pieces = 2
    piece_width = model_width // pieces
    normed_stream = lax.all_gather(normed_ffn, "tensor", axis=0, tiled=True)

    local_experts = expert_gate.shape[0]
    expert_count = local_experts * groups
    capacity = tok_dev * TOP // expert_count + tok_dev // 8
    id_blocks = expert_ids.reshape(groups, tok_dev, -1)
    gate_blocks = gate_weights.reshape(groups, tok_dev, -1)
    slots = jnp.arange(capacity, dtype=jnp.int32)
    onehots = []
    weights = []
    for local in range(local_experts):
        expert = position * local_experts + local
        chosen = id_blocks == expert
        hits = jnp.sum(chosen.astype(jnp.int32), axis=2)
        weights.append(jnp.sum(jnp.where(chosen, gate_blocks, 0.0), axis=2))
        rank = jnp.cumsum(hits, axis=1) - hits
        onehots.append(
            ((hits[:, None, :] > 0) & (rank[:, None, :] == slots[None, :, None])).astype(
                jnp.bfloat16
            )
        )

    shared_columns = jnp.concatenate([shared_gate, shared_up], axis=1)
    shared_width = shared_gate.shape[1]
    joined = jnp.dot(normed_stream, shared_columns, preferred_element_type=jnp.float32)
    token_blocks = normed_stream.reshape(groups, tok_dev, model_width)
    expert_gate_parts = []
    expert_up_parts = []
    for local in range(local_experts):
        picked = jnp.einsum(
            "bst,btd->bsd", onehots[local], token_blocks, preferred_element_type=jnp.float32
        ).astype(jnp.bfloat16).reshape(-1, model_width)
        expert_gate_parts.append(
            jnp.dot(picked, expert_gate[local], preferred_element_type=jnp.float32)
        )
        expert_up_parts.append(jnp.dot(picked, expert_up[local], preferred_element_type=jnp.float32))
    hidden_all = (jax.nn.silu(joined[:, :shared_width]) * joined[:, shared_width:]).astype(
        jnp.bfloat16
    )
    expert_hidden = [
        (jax.nn.silu(expert_gate_parts[local]) * expert_up_parts[local]).astype(jnp.bfloat16)
        for local in range(local_experts)
    ]

    outs = []
    for k in range(pieces):
        columns = slice(k * piece_width, (k + 1) * piece_width)
        term = jnp.dot(hidden_all, shared_down[:, columns], preferred_element_type=jnp.float32)
        for local in range(local_experts):
            rows = jnp.dot(
                expert_hidden[local], expert_down[local][:, columns], preferred_element_type=jnp.float32
            ).astype(jnp.bfloat16)
            back = jnp.einsum(
                "bst,bsd->btd",
                onehots[local],
                rows.reshape(groups, capacity, piece_width),
                preferred_element_type=jnp.float32,
            ).astype(jnp.bfloat16)
            term = term + weights[local].reshape(-1, 1) * back.reshape(-1, piece_width).astype(
                jnp.float32
            )
        outs.append(ring_reduce_scatter(term.astype(jnp.bfloat16), groups))
    ffn_out = jnp.concatenate(outs, axis=1)
    layer_out = (residual.astype(jnp.float32) + ffn_out).astype(jnp.bfloat16)
    return (layer_out, kv_pages)


def solution(mesh):
    placed = (
        P(("dp", "tensor"), None),
        P("dp"),
        P(),
        P(None, "tensor"),
        P(None, "tensor"),
        P(None, "tensor"),
        P("tensor", None),
        P(),
        P(None, "tensor"),
        P(None, "tensor"),
        P("tensor", None),
        P("tensor", None, None),
        P("tensor", None, None),
        P("tensor", None, None),
        P("dp", None),
        P("dp", None),
        P("dp"),
    )
    return jax.shard_map(
        shards,
        mesh=mesh,
        in_specs=placed,
        out_specs=(P(("dp", "tensor"), None), P(None, "dp", None, "tensor")),
        check_vma=False,
    )
```

```python
import jax
import jax.numpy as jnp
from jax import lax
from jax.sharding import PartitionSpec as P

HD = 128
TOP = 6
PAGE = 128


def rms_scale(hidden, gain):
    widened = hidden.astype(jnp.float32)
    inverse = lax.rsqrt(jnp.mean(widened * widened, axis=-1, keepdims=True) + 1e-06)
    return (widened * inverse * gain).astype(jnp.bfloat16)


def attend(projected, segment_ids, head_count):
    total_tokens = projected.shape[0]
    inner = head_count * HD
    queries = projected[:, :inner].reshape(total_tokens, head_count, HD)
    keys = projected[:, inner : 2 * inner].reshape(total_tokens, head_count, HD)
    values = projected[:, 2 * inner :].reshape(total_tokens, head_count, HD)
    scale = HD ** (-0.5)
    positions = jnp.arange(total_tokens, dtype=jnp.int32)
    span = min(512, total_tokens)

    def one_block(start):
        query_rows = lax.dynamic_slice_in_dim(queries, start, span, 0)
        query_segments = lax.dynamic_slice_in_dim(segment_ids, start, span, 0)
        query_positions = start + jnp.arange(span, dtype=jnp.int32)
        scores = (
            jnp.einsum("qhd,khd->hqk", query_rows, keys, preferred_element_type=jnp.float32) * scale
        )
        allowed = (query_segments[:, None] == segment_ids[None, :]) & (
            positions[None, :] <= query_positions[:, None]
        )
        scores = jnp.where(allowed[None], scores, -jnp.inf)
        highest = jnp.max(scores, axis=-1, keepdims=True)
        weights = jnp.exp(scores - highest)
        probs = (weights / jnp.sum(weights, axis=-1, keepdims=True)).astype(jnp.bfloat16)
        context = jnp.einsum("hqk,khd->qhd", probs, values, preferred_element_type=jnp.float32)
        return context.astype(jnp.bfloat16)

    starts = jnp.arange(total_tokens // span, dtype=jnp.int32) * span
    context = lax.map(one_block, starts).reshape(total_tokens, inner)
    return (context, keys.reshape(total_tokens, inner), values.reshape(total_tokens, inner))


def expert_apply(picked, gate_w, up_w, down_w):
    gate_part = jnp.dot(picked, gate_w, preferred_element_type=jnp.float32)
    upward = jnp.dot(picked, up_w, preferred_element_type=jnp.float32)
    hidden = (jax.nn.silu(gate_part) * upward).astype(jnp.bfloat16)
    return jnp.dot(hidden, down_w, preferred_element_type=jnp.float32).astype(jnp.bfloat16)


def ring_reduce_scatter(partial, groups):
    ring = groups // 4
    rows = partial.shape[0] // groups
    width = partial.shape[1]
    me = lax.axis_index("tensor")
    y = me // 4
    side = (me // 2) % 2
    core = me % 2
    blocks = partial.reshape(ring, 2, 2, rows, width)
    core_pairs = [(t, t ^ 1) for t in range(groups)]
    keep = lax.dynamic_index_in_dim(blocks, core, axis=2, keepdims=False)
    give = lax.dynamic_index_in_dim(blocks, 1 - core, axis=2, keepdims=False)
    got = lax.ppermute(give, "tensor", core_pairs)
    summed = keep.astype(jnp.float32) + got.astype(jnp.float32)
    half = width // 2
    forward_part = summed[..., :half]
    backward_part = summed[..., half:]
    forward_pairs = [(t, ((t // 4 + 1) % ring) * 4 + t % 4) for t in range(groups)]
    backward_pairs = [(t, ((t // 4 + ring - 1) % ring) * 4 + t % 4) for t in range(groups)]
    carry_f = lax.dynamic_index_in_dim(forward_part, (y + ring - 1) % ring, 0, False)
    carry_b = lax.dynamic_index_in_dim(backward_part, (y + 1) % ring, 0, False)
    carry_f = carry_f.astype(jnp.bfloat16)
    carry_b = carry_b.astype(jnp.bfloat16)
    for step in range(ring - 1):
        recv_f = lax.ppermute(carry_f, "tensor", forward_pairs)
        recv_b = lax.ppermute(carry_b, "tensor", backward_pairs)
        index_f = (y + 2 * ring - step - 2) % ring
        index_b = (y + step + 2) % ring
        acc_f = recv_f.astype(jnp.float32) + lax.dynamic_index_in_dim(
            forward_part, index_f, 0, False
        )
        acc_b = recv_b.astype(jnp.float32) + lax.dynamic_index_in_dim(
            backward_part, index_b, 0, False
        )
        carry_f = acc_f.astype(jnp.bfloat16)
        carry_b = acc_b.astype(jnp.bfloat16)
    mine = jnp.concatenate([acc_f, acc_b], axis=-1)
    side_pairs = [(t, t ^ 2) for t in range(groups)]
    keep_side = lax.dynamic_index_in_dim(mine, side, 0, False)
    give_side = lax.dynamic_index_in_dim(mine, 1 - side, 0, False).astype(jnp.bfloat16)
    got_side = lax.ppermute(give_side, "tensor", side_pairs)
    return keep_side + got_side.astype(jnp.float32)


def shards(
    tokens,
    segment_ids,
    attention_gain,
    query_weight,
    key_weight,
    value_weight,
    output_weight,
    ffn_gain,
    shared_gate,
    shared_up,
    shared_down,
    expert_gate,
    expert_up,
    expert_down,
    expert_ids,
    gate_weights,
    page_table,
):
    tok_dev = tokens.shape[0]
    groups = lax.axis_size("tensor")
    position = lax.axis_index("tensor")
    inner = query_weight.shape[1]
    head_count = inner // HD
    model_width = tokens.shape[1]

    projection = jnp.concatenate([query_weight, key_weight, value_weight], axis=1)
    normed_all = lax.all_gather(rms_scale(tokens, attention_gain), "tensor", axis=0, tiled=True)
    out_weight_all = lax.all_gather(output_weight, "tensor", axis=0, tiled=True)
    projected = lax.map(
        lambda rows: jnp.dot(rows, projection, preferred_element_type=jnp.float32).astype(
            jnp.bfloat16
        ),
        normed_all.reshape(4, -1, normed_all.shape[1]),
    ).reshape(normed_all.shape[0], -1)
    context, keys, values = attend(projected, segment_ids, head_count)
    cache = jnp.stack([keys, values]).reshape(2, -1, PAGE, inner)
    kv_pages = jnp.zeros_like(cache).at[:, page_table].set(cache)
    kv_pages, out_weight_all = lax.optimization_barrier((kv_pages, out_weight_all))

    received = lax.all_to_all(
        context.reshape(groups, tok_dev, inner), "tensor", split_axis=0, concat_axis=0, tiled=True
    )
    context_rows = received.transpose(1, 0, 2).reshape(tok_dev, groups * inner)
    attention = jnp.dot(context_rows, out_weight_all, preferred_element_type=jnp.float32)
    residual = (tokens.astype(jnp.float32) + attention).astype(jnp.bfloat16)
    normed_ffn = rms_scale(residual, ffn_gain)
    pieces = 2
    piece_width = model_width // pieces
    normed_stream = lax.all_gather(normed_ffn, "tensor", axis=0, tiled=True)

    local_experts = expert_gate.shape[0]
    expert_count = local_experts * groups
    capacity = tok_dev * TOP // expert_count + tok_dev // 8
    id_blocks = expert_ids.reshape(groups, tok_dev, -1)
    gate_blocks = gate_weights.reshape(groups, tok_dev, -1)
    slots = jnp.arange(capacity, dtype=jnp.int32)
    onehots = []
    weights = []
    for local in range(local_experts):
        expert = position * local_experts + local
        chosen = id_blocks == expert
        hits = jnp.sum(chosen.astype(jnp.int32), axis=2)
        weights.append(jnp.sum(jnp.where(chosen, gate_blocks, 0.0), axis=2))
        rank = jnp.cumsum(hits, axis=1) - hits
        onehots.append(
            ((hits[:, None, :] > 0) & (rank[:, None, :] == slots[None, :, None])).astype(
                jnp.bfloat16
            )
        )

    shared_columns = jnp.concatenate([shared_gate, shared_up], axis=1)
    shared_width = shared_gate.shape[1]
    joined = jnp.dot(normed_stream, shared_columns, preferred_element_type=jnp.float32)
    token_blocks = normed_stream.reshape(groups, tok_dev, model_width)
    expert_gate_parts = []
    expert_up_parts = []
    for local in range(local_experts):
        picked = jnp.einsum(
            "bst,btd->bsd", onehots[local], token_blocks, preferred_element_type=jnp.float32
        ).astype(jnp.bfloat16).reshape(-1, model_width)
        expert_gate_parts.append(
            jnp.dot(picked, expert_gate[local], preferred_element_type=jnp.float32)
        )
        expert_up_parts.append(jnp.dot(picked, expert_up[local], preferred_element_type=jnp.float32))
    hidden_all = (jax.nn.silu(joined[:, :shared_width]) * joined[:, shared_width:]).astype(
        jnp.bfloat16
    )
    expert_hidden = [
        (jax.nn.silu(expert_gate_parts[local]) * expert_up_parts[local]).astype(jnp.bfloat16)
        for local in range(local_experts)
    ]

    outs = []
    for k in range(pieces):
        columns = slice(k * piece_width, (k + 1) * piece_width)
        term = jnp.dot(hidden_all, shared_down[:, columns], preferred_element_type=jnp.float32)
        for local in range(local_experts):
            rows = jnp.dot(
                expert_hidden[local], expert_down[local][:, columns], preferred_element_type=jnp.float32
            ).astype(jnp.bfloat16)
            back = jnp.einsum(
                "bst,bsd->btd",
                onehots[local],
                rows.reshape(groups, capacity, piece_width),
                preferred_element_type=jnp.float32,
            ).astype(jnp.bfloat16)
            term = term + weights[local].reshape(-1, 1) * back.reshape(-1, piece_width).astype(
                jnp.float32
            )
        outs.append(ring_reduce_scatter(term.astype(jnp.bfloat16), groups))
    ffn_out = jnp.concatenate(outs, axis=1)
    layer_out = (residual.astype(jnp.float32) + ffn_out).astype(jnp.bfloat16)
    return (layer_out, kv_pages)


def solution(mesh):
    placed = (
        P(("dp", "tensor"), None),
        P("dp"),
        P(),
        P(None, "tensor"),
        P(None, "tensor"),
        P(None, "tensor"),
        P("tensor", None),
        P(),
        P(None, "tensor"),
        P(None, "tensor"),
        P("tensor", None),
        P("tensor", None, None),
        P("tensor", None, None),
        P("tensor", None, None),
        P("dp", None),
        P("dp", None),
        P("dp"),
    )
    return jax.shard_map(
        shards,
        mesh=mesh,
        in_specs=placed,
        out_specs=(P(("dp", "tensor"), None), P(None, "dp", None, "tensor")),
        check_vma=False,
    )
```

```python
import jax
import jax.numpy as jnp
from jax import lax
from jax.sharding import PartitionSpec as P

HD = 128
TOP = 6
PAGE = 128


def rms_scale(hidden, gain):
    widened = hidden.astype(jnp.float32)
    inverse = lax.rsqrt(jnp.mean(widened * widened, axis=-1, keepdims=True) + 1e-06)
    return (widened * inverse * gain).astype(jnp.bfloat16)


def attend(projected, segment_ids, head_count):
    total_tokens = projected.shape[0]
    inner = head_count * HD
    queries = projected[:, :inner].reshape(total_tokens, head_count, HD)
    keys = projected[:, inner : 2 * inner].reshape(total_tokens, head_count, HD)
    values = projected[:, 2 * inner :].reshape(total_tokens, head_count, HD)
    scale = HD ** (-0.5)
    positions = jnp.arange(total_tokens, dtype=jnp.int32)
    span = min(512, total_tokens)

    def one_block(start):
        query_rows = lax.dynamic_slice_in_dim(queries, start, span, 0)
        query_segments = lax.dynamic_slice_in_dim(segment_ids, start, span, 0)
        query_positions = start + jnp.arange(span, dtype=jnp.int32)
        scores = (
            jnp.einsum("qhd,khd->hqk", query_rows, keys, preferred_element_type=jnp.float32) * scale
        )
        allowed = (query_segments[:, None] == segment_ids[None, :]) & (
            positions[None, :] <= query_positions[:, None]
        )
        scores = jnp.where(allowed[None], scores, -jnp.inf)
        highest = jnp.max(scores, axis=-1, keepdims=True)
        weights = jnp.exp(scores - highest)
        probs = (weights / jnp.sum(weights, axis=-1, keepdims=True)).astype(jnp.bfloat16)
        context = jnp.einsum("hqk,khd->qhd", probs, values, preferred_element_type=jnp.float32)
        return context.astype(jnp.bfloat16)

    starts = jnp.arange(total_tokens // span, dtype=jnp.int32) * span
    context = lax.map(one_block, starts).reshape(total_tokens, inner)
    return (context, keys.reshape(total_tokens, inner), values.reshape(total_tokens, inner))


def expert_apply(picked, gate_w, up_w, down_w):
    gate_part = jnp.dot(picked, gate_w, preferred_element_type=jnp.float32)
    upward = jnp.dot(picked, up_w, preferred_element_type=jnp.float32)
    hidden = (jax.nn.silu(gate_part) * upward).astype(jnp.bfloat16)
    return jnp.dot(hidden, down_w, preferred_element_type=jnp.float32).astype(jnp.bfloat16)


def ring_reduce_scatter(partial, groups, direction):
    ring = groups // 4
    rows = partial.shape[0] // groups
    width = partial.shape[1]
    me = lax.axis_index("tensor")
    y = me // 4
    side = (me // 2) % 2
    core = me % 2
    blocks = partial.reshape(ring, 2, 2, rows, width)
    core_pairs = [(t, t ^ 1) for t in range(groups)]
    keep = lax.dynamic_index_in_dim(blocks, core, axis=2, keepdims=False)
    give = lax.dynamic_index_in_dim(blocks, 1 - core, axis=2, keepdims=False)
    got = lax.ppermute(give, "tensor", core_pairs)
    summed = keep.astype(jnp.float32) + got.astype(jnp.float32)
    ring_pairs = [(t, ((t // 4 + direction) % ring) * 4 + t % 4) for t in range(groups)]
    carry = lax.dynamic_index_in_dim(summed, (y + ring - direction) % ring, 0, False)
    carry = carry.astype(jnp.bfloat16)
    for step in range(ring - 1):
        received = lax.ppermute(carry, "tensor", ring_pairs)
        index = (y + 2 * ring - direction * (step + 2)) % ring
        acc = received.astype(jnp.float32) + lax.dynamic_index_in_dim(summed, index, 0, False)
        carry = acc.astype(jnp.bfloat16)
    side_pairs = [(t, t ^ 2) for t in range(groups)]
    keep_side = lax.dynamic_index_in_dim(acc, side, 0, False)
    give_side = lax.dynamic_index_in_dim(acc, 1 - side, 0, False).astype(jnp.bfloat16)
    got_side = lax.ppermute(give_side, "tensor", side_pairs)
    return keep_side + got_side.astype(jnp.float32)


def shards(
    tokens,
    segment_ids,
    attention_gain,
    query_weight,
    key_weight,
    value_weight,
    output_weight,
    ffn_gain,
    shared_gate,
    shared_up,
    shared_down,
    expert_gate,
    expert_up,
    expert_down,
    expert_ids,
    gate_weights,
    page_table,
):
    tok_dev = tokens.shape[0]
    groups = lax.axis_size("tensor")
    position = lax.axis_index("tensor")
    inner = query_weight.shape[1]
    head_count = inner // HD
    model_width = tokens.shape[1]

    projection = jnp.concatenate([query_weight, key_weight, value_weight], axis=1)
    normed_all = lax.all_gather(rms_scale(tokens, attention_gain), "tensor", axis=0, tiled=True)
    out_weight_all = lax.all_gather(output_weight, "tensor", axis=0, tiled=True)
    projected = lax.map(
        lambda rows: jnp.dot(rows, projection, preferred_element_type=jnp.float32).astype(
            jnp.bfloat16
        ),
        normed_all.reshape(4, -1, normed_all.shape[1]),
    ).reshape(normed_all.shape[0], -1)
    context, keys, values = attend(projected, segment_ids, head_count)
    cache = jnp.stack([keys, values]).reshape(2, -1, PAGE, inner)
    kv_pages = jnp.zeros_like(cache).at[:, page_table].set(cache)

    received = lax.all_to_all(
        context.reshape(groups, tok_dev, inner), "tensor", split_axis=0, concat_axis=0, tiled=True
    )
    context_rows = received.transpose(1, 0, 2).reshape(tok_dev, groups * inner)
    attention = jnp.dot(context_rows, out_weight_all, preferred_element_type=jnp.float32)
    residual = (tokens.astype(jnp.float32) + attention).astype(jnp.bfloat16)
    normed_ffn = rms_scale(residual, ffn_gain)
    pieces = 2
    piece_width = model_width // pieces
    normed_stream = lax.all_gather(normed_ffn, "tensor", axis=0, tiled=True)

    local_experts = expert_gate.shape[0]
    expert_count = local_experts * groups
    capacity = tok_dev * TOP // expert_count + tok_dev // 8
    id_blocks = expert_ids.reshape(groups, tok_dev, -1)
    gate_blocks = gate_weights.reshape(groups, tok_dev, -1)
    slots = jnp.arange(capacity, dtype=jnp.int32)
    onehots = []
    weights = []
    for local in range(local_experts):
        expert = position * local_experts + local
        chosen = id_blocks == expert
        hits = jnp.sum(chosen.astype(jnp.int32), axis=2)
        weights.append(jnp.sum(jnp.where(chosen, gate_blocks, 0.0), axis=2))
        rank = jnp.cumsum(hits, axis=1) - hits
        onehots.append(
            ((hits[:, None, :] > 0) & (rank[:, None, :] == slots[None, :, None])).astype(
                jnp.bfloat16
            )
        )

    shared_columns = jnp.concatenate([shared_gate, shared_up], axis=1)
    shared_width = shared_gate.shape[1]
    joined = jnp.dot(normed_stream, shared_columns, preferred_element_type=jnp.float32)
    token_blocks = normed_stream.reshape(groups, tok_dev, model_width)
    expert_gate_parts = []
    expert_up_parts = []
    for local in range(local_experts):
        picked = jnp.einsum(
            "bst,btd->bsd", onehots[local], token_blocks, preferred_element_type=jnp.float32
        ).astype(jnp.bfloat16).reshape(-1, model_width)
        expert_gate_parts.append(
            jnp.dot(picked, expert_gate[local], preferred_element_type=jnp.float32)
        )
        expert_up_parts.append(jnp.dot(picked, expert_up[local], preferred_element_type=jnp.float32))
    hidden_all = (jax.nn.silu(joined[:, :shared_width]) * joined[:, shared_width:]).astype(
        jnp.bfloat16
    )
    expert_hidden = [
        (jax.nn.silu(expert_gate_parts[local]) * expert_up_parts[local]).astype(jnp.bfloat16)
        for local in range(local_experts)
    ]

    outs = []
    for k in range(pieces):
        columns = slice(k * piece_width, (k + 1) * piece_width)
        term = jnp.dot(hidden_all, shared_down[:, columns], preferred_element_type=jnp.float32)
        for local in range(local_experts):
            rows = jnp.dot(
                expert_hidden[local], expert_down[local][:, columns], preferred_element_type=jnp.float32
            ).astype(jnp.bfloat16)
            back = jnp.einsum(
                "bst,bsd->btd",
                onehots[local],
                rows.reshape(groups, capacity, piece_width),
                preferred_element_type=jnp.float32,
            ).astype(jnp.bfloat16)
            term = term + weights[local].reshape(-1, 1) * back.reshape(-1, piece_width).astype(
                jnp.float32
            )
        outs.append(ring_reduce_scatter(term.astype(jnp.bfloat16), groups, 1 - 2 * (k % 2)))
    ffn_out = jnp.concatenate(outs, axis=1)
    layer_out = (residual.astype(jnp.float32) + ffn_out).astype(jnp.bfloat16)
    return (layer_out, kv_pages)


def solution(mesh):
    placed = (
        P(("dp", "tensor"), None),
        P("dp"),
        P(),
        P(None, "tensor"),
        P(None, "tensor"),
        P(None, "tensor"),
        P("tensor", None),
        P(),
        P(None, "tensor"),
        P(None, "tensor"),
        P("tensor", None),
        P("tensor", None, None),
        P("tensor", None, None),
        P("tensor", None, None),
        P("dp", None),
        P("dp", None),
        P("dp"),
    )
    return jax.shard_map(
        shards,
        mesh=mesh,
        in_specs=placed,
        out_specs=(P(("dp", "tensor"), None), P(None, "dp", None, "tensor")),
        check_vma=False,
    )
```

```python
import jax
import jax.numpy as jnp
from jax import lax
from jax.sharding import PartitionSpec as P

HD = 128
TOP = 6
PAGE = 128


def rms_scale(hidden, gain):
    widened = hidden.astype(jnp.float32)
    inverse = lax.rsqrt(jnp.mean(widened * widened, axis=-1, keepdims=True) + 1e-06)
    return (widened * inverse * gain).astype(jnp.bfloat16)


def attend(projected, segment_ids, head_count):
    total_tokens = projected.shape[0]
    inner = head_count * HD
    queries = projected[:, :inner].reshape(total_tokens, head_count, HD)
    keys = projected[:, inner : 2 * inner].reshape(total_tokens, head_count, HD)
    values = projected[:, 2 * inner :].reshape(total_tokens, head_count, HD)
    scale = HD ** (-0.5)
    positions = jnp.arange(total_tokens, dtype=jnp.int32)
    span = min(512, total_tokens)

    def one_block(start):
        query_rows = lax.dynamic_slice_in_dim(queries, start, span, 0)
        query_segments = lax.dynamic_slice_in_dim(segment_ids, start, span, 0)
        query_positions = start + jnp.arange(span, dtype=jnp.int32)
        scores = (
            jnp.einsum("qhd,khd->hqk", query_rows, keys, preferred_element_type=jnp.float32) * scale
        )
        allowed = (query_segments[:, None] == segment_ids[None, :]) & (
            positions[None, :] <= query_positions[:, None]
        )
        scores = jnp.where(allowed[None], scores, -jnp.inf)
        highest = jnp.max(scores, axis=-1, keepdims=True)
        weights = jnp.exp(scores - highest)
        probs = (weights / jnp.sum(weights, axis=-1, keepdims=True)).astype(jnp.bfloat16)
        context = jnp.einsum("hqk,khd->qhd", probs, values, preferred_element_type=jnp.float32)
        return context.astype(jnp.bfloat16)

    starts = jnp.arange(total_tokens // span, dtype=jnp.int32) * span
    context = lax.map(one_block, starts).reshape(total_tokens, inner)
    return (context, keys.reshape(total_tokens, inner), values.reshape(total_tokens, inner))


def expert_apply(picked, gate_w, up_w, down_w):
    gate_part = jnp.dot(picked, gate_w, preferred_element_type=jnp.float32)
    upward = jnp.dot(picked, up_w, preferred_element_type=jnp.float32)
    hidden = (jax.nn.silu(gate_part) * upward).astype(jnp.bfloat16)
    return jnp.dot(hidden, down_w, preferred_element_type=jnp.float32).astype(jnp.bfloat16)


def ring_reduce_scatter(partial, groups):
    ring = groups // 4
    rows = partial.shape[0] // groups
    width = partial.shape[1]
    me = lax.axis_index("tensor")
    y = me // 4
    side = (me // 2) % 2
    core = me % 2
    blocks = partial.reshape(ring, 2, 2, rows, width)
    core_pairs = [(t, t ^ 1) for t in range(groups)]
    keep = lax.dynamic_index_in_dim(blocks, core, axis=2, keepdims=False)
    give = lax.dynamic_index_in_dim(blocks, 1 - core, axis=2, keepdims=False)
    got = lax.ppermute(give, "tensor", core_pairs)
    summed = keep.astype(jnp.float32) + got.astype(jnp.float32)
    half = width // 2
    forward_part = summed[..., :half]
    backward_part = summed[..., half:]
    forward_pairs = [(t, ((t // 4 + 1) % ring) * 4 + t % 4) for t in range(groups)]
    backward_pairs = [(t, ((t // 4 + ring - 1) % ring) * 4 + t % 4) for t in range(groups)]
    carry_f = lax.dynamic_index_in_dim(forward_part, (y + ring - 1) % ring, 0, False)
    carry_b = lax.dynamic_index_in_dim(backward_part, (y + 1) % ring, 0, False)
    carry_f = carry_f.astype(jnp.bfloat16)
    carry_b = carry_b.astype(jnp.bfloat16)
    for step in range(ring - 1):
        recv_f = lax.ppermute(carry_f, "tensor", forward_pairs)
        recv_b = lax.ppermute(carry_b, "tensor", backward_pairs)
        index_f = (y + 2 * ring - step - 2) % ring
        index_b = (y + step + 2) % ring
        acc_f = recv_f.astype(jnp.float32) + lax.dynamic_index_in_dim(
            forward_part, index_f, 0, False
        )
        acc_b = recv_b.astype(jnp.float32) + lax.dynamic_index_in_dim(
            backward_part, index_b, 0, False
        )
        carry_f = acc_f.astype(jnp.bfloat16)
        carry_b = acc_b.astype(jnp.bfloat16)
    mine = jnp.concatenate([acc_f, acc_b], axis=-1)
    side_pairs = [(t, t ^ 2) for t in range(groups)]
    keep_side = lax.dynamic_index_in_dim(mine, side, 0, False)
    give_side = lax.dynamic_index_in_dim(mine, 1 - side, 0, False).astype(jnp.bfloat16)
    got_side = lax.ppermute(give_side, "tensor", side_pairs)
    return keep_side + got_side.astype(jnp.float32)


def shards(
    tokens,
    segment_ids,
    attention_gain,
    query_weight,
    key_weight,
    value_weight,
    output_weight,
    ffn_gain,
    shared_gate,
    shared_up,
    shared_down,
    expert_gate,
    expert_up,
    expert_down,
    expert_ids,
    gate_weights,
    page_table,
):
    tok_dev = tokens.shape[0]
    groups = lax.axis_size("tensor")
    position = lax.axis_index("tensor")
    inner = query_weight.shape[1]
    head_count = inner // HD
    model_width = tokens.shape[1]

    projection = jnp.concatenate([query_weight, key_weight, value_weight], axis=1)
    normed_all = lax.all_gather(rms_scale(tokens, attention_gain), "tensor", axis=0, tiled=True)
    out_weight_all = lax.all_gather(output_weight, "tensor", axis=0, tiled=True)
    projected = lax.map(
        lambda rows: jnp.dot(rows, projection, preferred_element_type=jnp.float32).astype(
            jnp.bfloat16
        ),
        normed_all.reshape(4, -1, normed_all.shape[1]),
    ).reshape(normed_all.shape[0], -1)
    context, keys, values = attend(projected, segment_ids, head_count)
    cache = jnp.stack([keys, values]).reshape(2, -1, PAGE, inner)
    kv_pages = jnp.zeros_like(cache).at[:, page_table].set(cache)

    received = lax.all_to_all(
        context.reshape(groups, tok_dev, inner), "tensor", split_axis=0, concat_axis=0, tiled=True
    )
    context_rows = received.transpose(1, 0, 2).reshape(tok_dev, groups * inner)
    attention = jnp.dot(context_rows, out_weight_all, preferred_element_type=jnp.float32)
    residual = (tokens.astype(jnp.float32) + attention).astype(jnp.bfloat16)
    normed_ffn = rms_scale(residual, ffn_gain)
    pieces = 2
    piece_width = model_width // pieces
    normed_stream = lax.all_gather(normed_ffn, "tensor", axis=0, tiled=True)

    local_experts = expert_gate.shape[0]
    expert_count = local_experts * groups
    capacity = tok_dev * TOP // expert_count + tok_dev // 8
    id_blocks = expert_ids.reshape(groups, tok_dev, -1)
    gate_blocks = gate_weights.reshape(groups, tok_dev, -1)
    slots = jnp.arange(capacity, dtype=jnp.int32)
    onehots = []
    weights = []
    for local in range(local_experts):
        expert = position * local_experts + local
        chosen = id_blocks == expert
        hits = jnp.sum(chosen.astype(jnp.int32), axis=2)
        weights.append(jnp.sum(jnp.where(chosen, gate_blocks, 0.0), axis=2))
        rank = jnp.cumsum(hits, axis=1) - hits
        onehots.append(
            ((hits[:, None, :] > 0) & (rank[:, None, :] == slots[None, :, None])).astype(
                jnp.bfloat16
            )
        )

    shared_columns = jnp.concatenate([shared_gate, shared_up], axis=1)
    shared_width = shared_gate.shape[1]
    joined = jnp.dot(normed_stream, shared_columns, preferred_element_type=jnp.float32)
    token_blocks = normed_stream.reshape(groups, tok_dev, model_width)
    expert_gate_parts = []
    expert_up_parts = []
    for local in range(local_experts):
        picked = jnp.einsum(
            "bst,btd->bsd", onehots[local], token_blocks, preferred_element_type=jnp.float32
        ).astype(jnp.bfloat16).reshape(-1, model_width)
        expert_gate_parts.append(
            jnp.dot(picked, expert_gate[local], preferred_element_type=jnp.float32)
        )
        expert_up_parts.append(jnp.dot(picked, expert_up[local], preferred_element_type=jnp.float32))
    hidden_all = (jax.nn.silu(joined[:, :shared_width]) * joined[:, shared_width:]).astype(
        jnp.bfloat16
    )
    expert_hidden = [
        (jax.nn.silu(expert_gate_parts[local]) * expert_up_parts[local]).astype(jnp.bfloat16)
        for local in range(local_experts)
    ]

    outs = []
    for k in range(pieces):
        columns = slice(k * piece_width, (k + 1) * piece_width)
        term = jnp.dot(hidden_all, shared_down[:, columns], preferred_element_type=jnp.float32)
        for local in range(local_experts):
            rows = jnp.dot(
                expert_hidden[local], expert_down[local][:, columns], preferred_element_type=jnp.float32
            ).astype(jnp.bfloat16)
            back = jnp.einsum(
                "bst,bsd->btd",
                onehots[local],
                rows.reshape(groups, capacity, piece_width),
                preferred_element_type=jnp.float32,
            ).astype(jnp.bfloat16)
            term = term + weights[local].reshape(-1, 1) * back.reshape(-1, piece_width).astype(
                jnp.float32
            )
        if k == 0:
            outs.append(
                lax.psum_scatter(
                    term.astype(jnp.bfloat16), "tensor", scatter_dimension=0, tiled=True
                ).astype(jnp.float32)
            )
        else:
            outs.append(ring_reduce_scatter(term.astype(jnp.bfloat16), groups))
    ffn_out = jnp.concatenate(outs, axis=1)
    layer_out = (residual.astype(jnp.float32) + ffn_out).astype(jnp.bfloat16)
    return (layer_out, kv_pages)


def solution(mesh):
    placed = (
        P(("dp", "tensor"), None),
        P("dp"),
        P(),
        P(None, "tensor"),
        P(None, "tensor"),
        P(None, "tensor"),
        P("tensor", None),
        P(),
        P(None, "tensor"),
        P(None, "tensor"),
        P("tensor", None),
        P("tensor", None, None),
        P("tensor", None, None),
        P("tensor", None, None),
        P("dp", None),
        P("dp", None),
        P("dp"),
    )
    return jax.shard_map(
        shards,
        mesh=mesh,
        in_specs=placed,
        out_specs=(P(("dp", "tensor"), None), P(None, "dp", None, "tensor")),
        check_vma=False,
    )
```

```python
import jax
import jax.numpy as jnp
from jax import lax
from jax.sharding import PartitionSpec as P

HD = 128
TOP = 6
PAGE = 128


def rms_scale(hidden, gain):
    widened = hidden.astype(jnp.float32)
    inverse = lax.rsqrt(jnp.mean(widened * widened, axis=-1, keepdims=True) + 1e-06)
    return (widened * inverse * gain).astype(jnp.bfloat16)


def attend(projected, segment_ids, head_count):
    total_tokens = projected.shape[0]
    inner = head_count * HD
    queries = projected[:, :inner].reshape(total_tokens, head_count, HD)
    keys = projected[:, inner : 2 * inner].reshape(total_tokens, head_count, HD)
    values = projected[:, 2 * inner :].reshape(total_tokens, head_count, HD)
    scale = HD ** (-0.5)
    positions = jnp.arange(total_tokens, dtype=jnp.int32)
    span = min(512, total_tokens)

    def one_block(start):
        query_rows = lax.dynamic_slice_in_dim(queries, start, span, 0)
        query_segments = lax.dynamic_slice_in_dim(segment_ids, start, span, 0)
        query_positions = start + jnp.arange(span, dtype=jnp.int32)
        scores = (
            jnp.einsum("qhd,khd->hqk", query_rows, keys, preferred_element_type=jnp.float32) * scale
        )
        allowed = (query_segments[:, None] == segment_ids[None, :]) & (
            positions[None, :] <= query_positions[:, None]
        )
        scores = jnp.where(allowed[None], scores, -jnp.inf)
        highest = jnp.max(scores, axis=-1, keepdims=True)
        weights = jnp.exp(scores - highest)
        probs = (weights / jnp.sum(weights, axis=-1, keepdims=True)).astype(jnp.bfloat16)
        context = jnp.einsum("hqk,khd->qhd", probs, values, preferred_element_type=jnp.float32)
        return context.astype(jnp.bfloat16)

    starts = jnp.arange(total_tokens // span, dtype=jnp.int32) * span
    context = lax.map(one_block, starts).reshape(total_tokens, inner)
    return (context, keys.reshape(total_tokens, inner), values.reshape(total_tokens, inner))


def expert_apply(picked, gate_w, up_w, down_w):
    gate_part = jnp.dot(picked, gate_w, preferred_element_type=jnp.float32)
    upward = jnp.dot(picked, up_w, preferred_element_type=jnp.float32)
    hidden = (jax.nn.silu(gate_part) * upward).astype(jnp.bfloat16)
    return jnp.dot(hidden, down_w, preferred_element_type=jnp.float32).astype(jnp.bfloat16)


def ring_reduce_scatter(partial, groups):
    ring = groups // 4
    rows = partial.shape[0] // groups
    width = partial.shape[1]
    me = lax.axis_index("tensor")
    y = me // 4
    side = (me // 2) % 2
    core = me % 2
    blocks = partial.reshape(ring, 2, 2, rows, width)
    core_pairs = [(t, t ^ 1) for t in range(groups)]
    keep = lax.dynamic_index_in_dim(blocks, core, axis=2, keepdims=False)
    give = lax.dynamic_index_in_dim(blocks, 1 - core, axis=2, keepdims=False)
    got = lax.ppermute(give, "tensor", core_pairs)
    summed = keep.astype(jnp.float32) + got.astype(jnp.float32)
    forward_pairs = [(t, ((t // 4 + 1) % ring) * 4 + t % 4) for t in range(groups)]
    backward_pairs = [(t, ((t // 4 + ring - 1) % ring) * 4 + t % 4) for t in range(groups)]
    half = width // 2
    own = lax.dynamic_index_in_dim(summed, y, 0, False)
    to_next = lax.dynamic_index_in_dim(summed, (y + 1) % ring, 0, False)
    to_prev = lax.dynamic_index_in_dim(summed, (y + ring - 1) % ring, 0, False)
    far = lax.dynamic_index_in_dim(summed, (y + 2) % ring, 0, False)
    send_f = jnp.concatenate([to_next, far[..., :half]], axis=-1).astype(jnp.bfloat16)
    send_b = jnp.concatenate([to_prev, far[..., half:]], axis=-1).astype(jnp.bfloat16)
    recv_f = lax.ppermute(send_f, "tensor", forward_pairs)
    recv_b = lax.ppermute(send_b, "tensor", backward_pairs)
    relay_f = lax.ppermute(recv_f[..., width:], "tensor", forward_pairs)
    relay_b = lax.ppermute(recv_b[..., width:], "tensor", backward_pairs)
    acc = (
        own
        + recv_f[..., :width].astype(jnp.float32)
        + recv_b[..., :width].astype(jnp.float32)
        + jnp.concatenate([relay_f, relay_b], axis=-1).astype(jnp.float32)
    )
    side_pairs = [(t, t ^ 2) for t in range(groups)]
    keep_side = lax.dynamic_index_in_dim(acc, side, 0, False)
    give_side = lax.dynamic_index_in_dim(acc, 1 - side, 0, False).astype(jnp.bfloat16)
    got_side = lax.ppermute(give_side, "tensor", side_pairs)
    return keep_side + got_side.astype(jnp.float32)


def shards(
    tokens,
    segment_ids,
    attention_gain,
    query_weight,
    key_weight,
    value_weight,
    output_weight,
    ffn_gain,
    shared_gate,
    shared_up,
    shared_down,
    expert_gate,
    expert_up,
    expert_down,
    expert_ids,
    gate_weights,
    page_table,
):
    tok_dev = tokens.shape[0]
    groups = lax.axis_size("tensor")
    position = lax.axis_index("tensor")
    inner = query_weight.shape[1]
    head_count = inner // HD
    model_width = tokens.shape[1]

    projection = jnp.concatenate([query_weight, key_weight, value_weight], axis=1)
    normed_all = lax.all_gather(rms_scale(tokens, attention_gain), "tensor", axis=0, tiled=True)
    out_weight_all = lax.all_gather(output_weight, "tensor", axis=0, tiled=True)
    projected = lax.map(
        lambda rows: jnp.dot(rows, projection, preferred_element_type=jnp.float32).astype(
            jnp.bfloat16
        ),
        normed_all.reshape(4, -1, normed_all.shape[1]),
    ).reshape(normed_all.shape[0], -1)
    context, keys, values = attend(projected, segment_ids, head_count)
    cache = jnp.stack([keys, values]).reshape(2, -1, PAGE, inner)
    kv_pages = jnp.zeros_like(cache).at[:, page_table].set(cache)

    received = lax.all_to_all(
        context.reshape(groups, tok_dev, inner), "tensor", split_axis=0, concat_axis=0, tiled=True
    )
    context_rows = received.transpose(1, 0, 2).reshape(tok_dev, groups * inner)
    attention = jnp.dot(context_rows, out_weight_all, preferred_element_type=jnp.float32)
    residual = (tokens.astype(jnp.float32) + attention).astype(jnp.bfloat16)
    normed_ffn = rms_scale(residual, ffn_gain)
    pieces = 2
    piece_width = model_width // pieces
    normed_stream = lax.all_gather(normed_ffn, "tensor", axis=0, tiled=True)

    local_experts = expert_gate.shape[0]
    expert_count = local_experts * groups
    capacity = tok_dev * TOP // expert_count + tok_dev // 8
    id_blocks = expert_ids.reshape(groups, tok_dev, -1)
    gate_blocks = gate_weights.reshape(groups, tok_dev, -1)
    slots = jnp.arange(capacity, dtype=jnp.int32)
    onehots = []
    weights = []
    for local in range(local_experts):
        expert = position * local_experts + local
        chosen = id_blocks == expert
        hits = jnp.sum(chosen.astype(jnp.int32), axis=2)
        weights.append(jnp.sum(jnp.where(chosen, gate_blocks, 0.0), axis=2))
        rank = jnp.cumsum(hits, axis=1) - hits
        onehots.append(
            ((hits[:, None, :] > 0) & (rank[:, None, :] == slots[None, :, None])).astype(
                jnp.bfloat16
            )
        )

    shared_columns = jnp.concatenate([shared_gate, shared_up], axis=1)
    shared_width = shared_gate.shape[1]
    joined = jnp.dot(normed_stream, shared_columns, preferred_element_type=jnp.float32)
    token_blocks = normed_stream.reshape(groups, tok_dev, model_width)
    expert_gate_parts = []
    expert_up_parts = []
    for local in range(local_experts):
        picked = jnp.einsum(
            "bst,btd->bsd", onehots[local], token_blocks, preferred_element_type=jnp.float32
        ).astype(jnp.bfloat16).reshape(-1, model_width)
        expert_gate_parts.append(
            jnp.dot(picked, expert_gate[local], preferred_element_type=jnp.float32)
        )
        expert_up_parts.append(jnp.dot(picked, expert_up[local], preferred_element_type=jnp.float32))
    hidden_all = (jax.nn.silu(joined[:, :shared_width]) * joined[:, shared_width:]).astype(
        jnp.bfloat16
    )
    expert_hidden = [
        (jax.nn.silu(expert_gate_parts[local]) * expert_up_parts[local]).astype(jnp.bfloat16)
        for local in range(local_experts)
    ]

    outs = []
    for k in range(pieces):
        columns = slice(k * piece_width, (k + 1) * piece_width)
        term = jnp.dot(hidden_all, shared_down[:, columns], preferred_element_type=jnp.float32)
        for local in range(local_experts):
            rows = jnp.dot(
                expert_hidden[local], expert_down[local][:, columns], preferred_element_type=jnp.float32
            ).astype(jnp.bfloat16)
            back = jnp.einsum(
                "bst,bsd->btd",
                onehots[local],
                rows.reshape(groups, capacity, piece_width),
                preferred_element_type=jnp.float32,
            ).astype(jnp.bfloat16)
            term = term + weights[local].reshape(-1, 1) * back.reshape(-1, piece_width).astype(
                jnp.float32
            )
        outs.append(ring_reduce_scatter(term.astype(jnp.bfloat16), groups))
    ffn_out = jnp.concatenate(outs, axis=1)
    layer_out = (residual.astype(jnp.float32) + ffn_out).astype(jnp.bfloat16)
    return (layer_out, kv_pages)


def solution(mesh):
    placed = (
        P(("dp", "tensor"), None),
        P("dp"),
        P(),
        P(None, "tensor"),
        P(None, "tensor"),
        P(None, "tensor"),
        P("tensor", None),
        P(),
        P(None, "tensor"),
        P(None, "tensor"),
        P("tensor", None),
        P("tensor", None, None),
        P("tensor", None, None),
        P("tensor", None, None),
        P("dp", None),
        P("dp", None),
        P("dp"),
    )
    return jax.shard_map(
        shards,
        mesh=mesh,
        in_specs=placed,
        out_specs=(P(("dp", "tensor"), None), P(None, "dp", None, "tensor")),
        check_vma=False,
    )
```

```python
import jax
import jax.numpy as jnp
from jax import lax
from jax.sharding import PartitionSpec as P

HD = 128
TOP = 6
PAGE = 128


def rms_scale(hidden, gain):
    widened = hidden.astype(jnp.float32)
    inverse = lax.rsqrt(jnp.mean(widened * widened, axis=-1, keepdims=True) + 1e-06)
    return (widened * inverse * gain).astype(jnp.bfloat16)


def attend(projected, segment_ids, head_count):
    total_tokens = projected.shape[0]
    inner = head_count * HD
    queries = projected[:, :inner].reshape(total_tokens, head_count, HD)
    keys = projected[:, inner : 2 * inner].reshape(total_tokens, head_count, HD)
    values = projected[:, 2 * inner :].reshape(total_tokens, head_count, HD)
    scale = HD ** (-0.5)
    positions = jnp.arange(total_tokens, dtype=jnp.int32)
    span = min(512, total_tokens)

    def one_block(start):
        query_rows = lax.dynamic_slice_in_dim(queries, start, span, 0)
        query_segments = lax.dynamic_slice_in_dim(segment_ids, start, span, 0)
        query_positions = start + jnp.arange(span, dtype=jnp.int32)
        scores = (
            jnp.einsum("qhd,khd->hqk", query_rows, keys, preferred_element_type=jnp.float32) * scale
        )
        allowed = (query_segments[:, None] == segment_ids[None, :]) & (
            positions[None, :] <= query_positions[:, None]
        )
        scores = jnp.where(allowed[None], scores, -jnp.inf)
        highest = jnp.max(scores, axis=-1, keepdims=True)
        weights = jnp.exp(scores - highest)
        probs = (weights / jnp.sum(weights, axis=-1, keepdims=True)).astype(jnp.bfloat16)
        context = jnp.einsum("hqk,khd->qhd", probs, values, preferred_element_type=jnp.float32)
        return context.astype(jnp.bfloat16)

    starts = jnp.arange(total_tokens // span, dtype=jnp.int32) * span
    context = lax.map(one_block, starts).reshape(total_tokens, inner)
    return (context, keys.reshape(total_tokens, inner), values.reshape(total_tokens, inner))


def expert_apply(picked, gate_w, up_w, down_w):
    gate_part = jnp.dot(picked, gate_w, preferred_element_type=jnp.float32)
    upward = jnp.dot(picked, up_w, preferred_element_type=jnp.float32)
    hidden = (jax.nn.silu(gate_part) * upward).astype(jnp.bfloat16)
    return jnp.dot(hidden, down_w, preferred_element_type=jnp.float32).astype(jnp.bfloat16)


def ring_reduce_scatter(partial, groups, x_first):
    ring = groups // 4
    rows = partial.shape[0] // groups
    width = partial.shape[1]
    me = lax.axis_index("tensor")
    y = me // 4
    side = (me // 2) % 2
    core = me % 2
    blocks = partial.reshape(ring, 2, 2, rows, width)
    core_pairs = [(t, t ^ 1) for t in range(groups)]
    side_pairs = [(t, t ^ 2) for t in range(groups)]
    keep = lax.dynamic_index_in_dim(blocks, core, axis=2, keepdims=False)
    give = lax.dynamic_index_in_dim(blocks, 1 - core, axis=2, keepdims=False)
    got = lax.ppermute(give, "tensor", core_pairs)
    summed = keep.astype(jnp.float32) + got.astype(jnp.float32)
    if x_first:
        keep_side = lax.dynamic_index_in_dim(summed, side, 1, False)
        give_side = lax.dynamic_index_in_dim(summed, 1 - side, 1, False).astype(jnp.bfloat16)
        got_side = lax.ppermute(give_side, "tensor", side_pairs)
        summed = keep_side + got_side.astype(jnp.float32)
    half = width // 2
    forward_part = summed[..., :half]
    backward_part = summed[..., half:]
    forward_pairs = [(t, ((t // 4 + 1) % ring) * 4 + t % 4) for t in range(groups)]
    backward_pairs = [(t, ((t // 4 + ring - 1) % ring) * 4 + t % 4) for t in range(groups)]
    carry_f = lax.dynamic_index_in_dim(forward_part, (y + ring - 1) % ring, 0, False)
    carry_b = lax.dynamic_index_in_dim(backward_part, (y + 1) % ring, 0, False)
    carry_f = carry_f.astype(jnp.bfloat16)
    carry_b = carry_b.astype(jnp.bfloat16)
    for step in range(ring - 1):
        recv_f = lax.ppermute(carry_f, "tensor", forward_pairs)
        recv_b = lax.ppermute(carry_b, "tensor", backward_pairs)
        index_f = (y + 2 * ring - step - 2) % ring
        index_b = (y + step + 2) % ring
        acc_f = recv_f.astype(jnp.float32) + lax.dynamic_index_in_dim(
            forward_part, index_f, 0, False
        )
        acc_b = recv_b.astype(jnp.float32) + lax.dynamic_index_in_dim(
            backward_part, index_b, 0, False
        )
        carry_f = acc_f.astype(jnp.bfloat16)
        carry_b = acc_b.astype(jnp.bfloat16)
    mine = jnp.concatenate([acc_f, acc_b], axis=-1)
    if x_first:
        return mine
    keep_side = lax.dynamic_index_in_dim(mine, side, 0, False)
    give_side = lax.dynamic_index_in_dim(mine, 1 - side, 0, False).astype(jnp.bfloat16)
    got_side = lax.ppermute(give_side, "tensor", side_pairs)
    return keep_side + got_side.astype(jnp.float32)


def shards(
    tokens,
    segment_ids,
    attention_gain,
    query_weight,
    key_weight,
    value_weight,
    output_weight,
    ffn_gain,
    shared_gate,
    shared_up,
    shared_down,
    expert_gate,
    expert_up,
    expert_down,
    expert_ids,
    gate_weights,
    page_table,
):
    tok_dev = tokens.shape[0]
    groups = lax.axis_size("tensor")
    position = lax.axis_index("tensor")
    inner = query_weight.shape[1]
    head_count = inner // HD
    model_width = tokens.shape[1]

    projection = jnp.concatenate([query_weight, key_weight, value_weight], axis=1)
    normed_all = lax.all_gather(rms_scale(tokens, attention_gain), "tensor", axis=0, tiled=True)
    out_weight_all = lax.all_gather(output_weight, "tensor", axis=0, tiled=True)
    projected = lax.map(
        lambda rows: jnp.dot(rows, projection, preferred_element_type=jnp.float32).astype(
            jnp.bfloat16
        ),
        normed_all.reshape(4, -1, normed_all.shape[1]),
    ).reshape(normed_all.shape[0], -1)
    context, keys, values = attend(projected, segment_ids, head_count)
    cache = jnp.stack([keys, values]).reshape(2, -1, PAGE, inner)
    kv_pages = jnp.zeros_like(cache).at[:, page_table].set(cache)

    received = lax.all_to_all(
        context.reshape(groups, tok_dev, inner), "tensor", split_axis=0, concat_axis=0, tiled=True
    )
    context_rows = received.transpose(1, 0, 2).reshape(tok_dev, groups * inner)
    attention = jnp.dot(context_rows, out_weight_all, preferred_element_type=jnp.float32)
    residual = (tokens.astype(jnp.float32) + attention).astype(jnp.bfloat16)
    normed_ffn = rms_scale(residual, ffn_gain)
    pieces = 2
    piece_width = model_width // pieces
    normed_stream = lax.all_gather(normed_ffn, "tensor", axis=0, tiled=True)

    local_experts = expert_gate.shape[0]
    expert_count = local_experts * groups
    capacity = tok_dev * TOP // expert_count + tok_dev // 8
    id_blocks = expert_ids.reshape(groups, tok_dev, -1)
    gate_blocks = gate_weights.reshape(groups, tok_dev, -1)
    slots = jnp.arange(capacity, dtype=jnp.int32)
    onehots = []
    weights = []
    for local in range(local_experts):
        expert = position * local_experts + local
        chosen = id_blocks == expert
        hits = jnp.sum(chosen.astype(jnp.int32), axis=2)
        weights.append(jnp.sum(jnp.where(chosen, gate_blocks, 0.0), axis=2))
        rank = jnp.cumsum(hits, axis=1) - hits
        onehots.append(
            ((hits[:, None, :] > 0) & (rank[:, None, :] == slots[None, :, None])).astype(
                jnp.bfloat16
            )
        )

    shared_columns = jnp.concatenate([shared_gate, shared_up], axis=1)
    shared_width = shared_gate.shape[1]
    joined = jnp.dot(normed_stream, shared_columns, preferred_element_type=jnp.float32)
    token_blocks = normed_stream.reshape(groups, tok_dev, model_width)
    expert_gate_parts = []
    expert_up_parts = []
    for local in range(local_experts):
        picked = jnp.einsum(
            "bst,btd->bsd", onehots[local], token_blocks, preferred_element_type=jnp.float32
        ).astype(jnp.bfloat16).reshape(-1, model_width)
        expert_gate_parts.append(
            jnp.dot(picked, expert_gate[local], preferred_element_type=jnp.float32)
        )
        expert_up_parts.append(jnp.dot(picked, expert_up[local], preferred_element_type=jnp.float32))
    hidden_all = (jax.nn.silu(joined[:, :shared_width]) * joined[:, shared_width:]).astype(
        jnp.bfloat16
    )
    expert_hidden = [
        (jax.nn.silu(expert_gate_parts[local]) * expert_up_parts[local]).astype(jnp.bfloat16)
        for local in range(local_experts)
    ]

    outs = []
    for k in range(pieces):
        columns = slice(k * piece_width, (k + 1) * piece_width)
        term = jnp.dot(hidden_all, shared_down[:, columns], preferred_element_type=jnp.float32)
        for local in range(local_experts):
            rows = jnp.dot(
                expert_hidden[local], expert_down[local][:, columns], preferred_element_type=jnp.float32
            ).astype(jnp.bfloat16)
            back = jnp.einsum(
                "bst,bsd->btd",
                onehots[local],
                rows.reshape(groups, capacity, piece_width),
                preferred_element_type=jnp.float32,
            ).astype(jnp.bfloat16)
            term = term + weights[local].reshape(-1, 1) * back.reshape(-1, piece_width).astype(
                jnp.float32
            )
        outs.append(ring_reduce_scatter(term.astype(jnp.bfloat16), groups, k % 2 == 1))
    ffn_out = jnp.concatenate(outs, axis=1)
    layer_out = (residual.astype(jnp.float32) + ffn_out).astype(jnp.bfloat16)
    return (layer_out, kv_pages)


def solution(mesh):
    placed = (
        P(("dp", "tensor"), None),
        P("dp"),
        P(),
        P(None, "tensor"),
        P(None, "tensor"),
        P(None, "tensor"),
        P("tensor", None),
        P(),
        P(None, "tensor"),
        P(None, "tensor"),
        P("tensor", None),
        P("tensor", None, None),
        P("tensor", None, None),
        P("tensor", None, None),
        P("dp", None),
        P("dp", None),
        P("dp"),
    )
    return jax.shard_map(
        shards,
        mesh=mesh,
        in_specs=placed,
        out_specs=(P(("dp", "tensor"), None), P(None, "dp", None, "tensor")),
        check_vma=False,
    )
```

```python
import jax
import jax.numpy as jnp
from jax import lax
from jax.sharding import PartitionSpec as P

HD = 128
TOP = 6
PAGE = 128


def rms_scale(hidden, gain):
    widened = hidden.astype(jnp.float32)
    inverse = lax.rsqrt(jnp.mean(widened * widened, axis=-1, keepdims=True) + 1e-06)
    return (widened * inverse * gain).astype(jnp.bfloat16)


def attend(projected, segment_ids, head_count):
    total_tokens = projected.shape[0]
    inner = head_count * HD
    queries = projected[:, :inner].reshape(total_tokens, head_count, HD)
    keys = projected[:, inner : 2 * inner].reshape(total_tokens, head_count, HD)
    values = projected[:, 2 * inner :].reshape(total_tokens, head_count, HD)
    scale = HD ** (-0.5)
    positions = jnp.arange(total_tokens, dtype=jnp.int32)
    span = min(512, total_tokens)

    def one_block(start):
        query_rows = lax.dynamic_slice_in_dim(queries, start, span, 0)
        query_segments = lax.dynamic_slice_in_dim(segment_ids, start, span, 0)
        query_positions = start + jnp.arange(span, dtype=jnp.int32)
        scores = (
            jnp.einsum("qhd,khd->hqk", query_rows, keys, preferred_element_type=jnp.float32) * scale
        )
        allowed = (query_segments[:, None] == segment_ids[None, :]) & (
            positions[None, :] <= query_positions[:, None]
        )
        scores = jnp.where(allowed[None], scores, -jnp.inf)
        highest = jnp.max(scores, axis=-1, keepdims=True)
        weights = jnp.exp(scores - highest)
        probs = (weights / jnp.sum(weights, axis=-1, keepdims=True)).astype(jnp.bfloat16)
        context = jnp.einsum("hqk,khd->qhd", probs, values, preferred_element_type=jnp.float32)
        return context.astype(jnp.bfloat16)

    starts = jnp.arange(total_tokens // span, dtype=jnp.int32) * span
    context = lax.map(one_block, starts).reshape(total_tokens, inner)
    return (context, keys.reshape(total_tokens, inner), values.reshape(total_tokens, inner))


def expert_apply(picked, gate_w, up_w, down_w):
    gate_part = jnp.dot(picked, gate_w, preferred_element_type=jnp.float32)
    upward = jnp.dot(picked, up_w, preferred_element_type=jnp.float32)
    hidden = (jax.nn.silu(gate_part) * upward).astype(jnp.bfloat16)
    return jnp.dot(hidden, down_w, preferred_element_type=jnp.float32).astype(jnp.bfloat16)


def ring_reduce_scatter(partial, groups):
    ring = groups // 4
    rows = partial.shape[0] // groups
    width = partial.shape[1]
    me = lax.axis_index("tensor")
    y = me // 4
    side = (me // 2) % 2
    core = me % 2
    blocks = partial.reshape(ring, 2, 2, rows, width)
    core_pairs = [(t, t ^ 1) for t in range(groups)]
    keep = lax.dynamic_index_in_dim(blocks, core, axis=2, keepdims=False)
    give = lax.dynamic_index_in_dim(blocks, 1 - core, axis=2, keepdims=False)
    got = lax.ppermute(give, "tensor", core_pairs)
    summed = keep.astype(jnp.float32) + got.astype(jnp.float32)
    half = width // 2
    forward_part = summed[..., :half]
    backward_part = summed[..., half:]
    forward_pairs = [(t, ((t // 4 + 1) % ring) * 4 + t % 4) for t in range(groups)]
    backward_pairs = [(t, ((t // 4 + ring - 1) % ring) * 4 + t % 4) for t in range(groups)]
    carry_f = lax.dynamic_index_in_dim(forward_part, (y + ring - 1) % ring, 0, False)
    carry_b = lax.dynamic_index_in_dim(backward_part, (y + 1) % ring, 0, False)
    carry_f = carry_f.astype(jnp.bfloat16)
    carry_b = carry_b.astype(jnp.bfloat16)
    for step in range(ring - 1):
        recv_f = lax.ppermute(carry_f, "tensor", forward_pairs)
        recv_b = lax.ppermute(carry_b, "tensor", backward_pairs)
        index_f = (y + 2 * ring - step - 2) % ring
        index_b = (y + step + 2) % ring
        acc_f = recv_f.astype(jnp.float32) + lax.dynamic_index_in_dim(
            forward_part, index_f, 0, False
        )
        acc_b = recv_b.astype(jnp.float32) + lax.dynamic_index_in_dim(
            backward_part, index_b, 0, False
        )
        carry_f = acc_f.astype(jnp.bfloat16)
        carry_b = acc_b.astype(jnp.bfloat16)
    mine = jnp.concatenate([acc_f, acc_b], axis=-1)
    side_pairs = [(t, t ^ 2) for t in range(groups)]
    keep_side = lax.dynamic_index_in_dim(mine, side, 0, False)
    give_side = lax.dynamic_index_in_dim(mine, 1 - side, 0, False).astype(jnp.bfloat16)
    got_side = lax.ppermute(give_side, "tensor", side_pairs)
    return keep_side + got_side.astype(jnp.float32)


def shards(
    tokens,
    segment_ids,
    attention_gain,
    query_weight,
    key_weight,
    value_weight,
    output_weight,
    ffn_gain,
    shared_gate,
    shared_up,
    shared_down,
    expert_gate,
    expert_up,
    expert_down,
    expert_ids,
    gate_weights,
    page_table,
):
    tok_dev = tokens.shape[0]
    groups = lax.axis_size("tensor")
    position = lax.axis_index("tensor")
    inner = query_weight.shape[1]
    head_count = inner // HD
    model_width = tokens.shape[1]

    projection = jnp.concatenate([query_weight, key_weight, value_weight], axis=1)
    normed_all = lax.all_gather(rms_scale(tokens, attention_gain), "tensor", axis=0, tiled=True)
    out_weight_all = lax.all_gather(output_weight, "tensor", axis=0, tiled=True)
    projected = lax.map(
        lambda rows: jnp.dot(rows, projection, preferred_element_type=jnp.float32).astype(
            jnp.bfloat16
        ),
        normed_all.reshape(4, -1, normed_all.shape[1]),
    ).reshape(normed_all.shape[0], -1)
    context, keys, values = attend(projected, segment_ids, head_count)
    cache = jnp.stack([keys, values]).reshape(2, -1, PAGE, inner)
    kv_pages = jnp.zeros_like(cache).at[:, page_table].set(cache)

    received = lax.all_to_all(
        context.reshape(groups, tok_dev, inner), "tensor", split_axis=0, concat_axis=0, tiled=True
    )
    context_rows = received.transpose(1, 0, 2).reshape(tok_dev, groups * inner)
    attention = jnp.dot(context_rows, out_weight_all, preferred_element_type=jnp.float32)
    residual = (tokens.astype(jnp.float32) + attention).astype(jnp.bfloat16)
    normed_ffn = rms_scale(residual, ffn_gain)
    pieces = 2
    piece_width = model_width // pieces
    normed_stream = lax.all_gather(normed_ffn, "tensor", axis=0, tiled=True)

    local_experts = expert_gate.shape[0]
    expert_count = local_experts * groups
    capacity = tok_dev * TOP // expert_count + tok_dev // 8
    id_blocks = expert_ids.reshape(groups, tok_dev, -1)
    gate_blocks = gate_weights.reshape(groups, tok_dev, -1)
    slots = jnp.arange(capacity, dtype=jnp.int32)
    onehots = []
    weights = []
    for local in range(local_experts):
        expert = position * local_experts + local
        chosen = id_blocks == expert
        hits = jnp.sum(chosen.astype(jnp.int32), axis=2)
        weights.append(jnp.sum(jnp.where(chosen, gate_blocks, 0.0), axis=2))
        rank = jnp.cumsum(hits, axis=1) - hits
        onehots.append(
            ((hits[:, None, :] > 0) & (rank[:, None, :] == slots[None, :, None])).astype(
                jnp.bfloat16
            )
        )

    shared_columns = jnp.concatenate([shared_gate, shared_up], axis=1)
    shared_width = shared_gate.shape[1]
    joined = jnp.dot(normed_stream, shared_columns, preferred_element_type=jnp.float32)
    token_blocks = normed_stream.reshape(groups, tok_dev, model_width)
    hidden_all = (jax.nn.silu(joined[:, :shared_width]) * joined[:, shared_width:]).astype(
        jnp.bfloat16
    )
    expert_hidden = []
    for local in range(local_experts):
        picked = jnp.einsum(
            "bst,btd->bsd", onehots[local], token_blocks, preferred_element_type=jnp.float32
        ).astype(jnp.bfloat16)
        gate_w = expert_gate[local]
        up_w = expert_up[local]

        def hidden_rows(rows):
            gate_part = jnp.dot(rows, gate_w, preferred_element_type=jnp.float32)
            upward = jnp.dot(rows, up_w, preferred_element_type=jnp.float32)
            return (jax.nn.silu(gate_part) * upward).astype(jnp.bfloat16)

        expert_hidden.append(
            lax.map(hidden_rows, picked.reshape(4, -1, model_width)).reshape(
                groups * capacity, -1
            )
        )

    outs = []
    for k in range(pieces):
        columns = slice(k * piece_width, (k + 1) * piece_width)
        term = jnp.dot(hidden_all, shared_down[:, columns], preferred_element_type=jnp.float32)
        for local in range(local_experts):
            rows = jnp.dot(
                expert_hidden[local], expert_down[local][:, columns], preferred_element_type=jnp.float32
            ).astype(jnp.bfloat16)
            back = jnp.einsum(
                "bst,bsd->btd",
                onehots[local],
                rows.reshape(groups, capacity, piece_width),
                preferred_element_type=jnp.float32,
            ).astype(jnp.bfloat16)
            term = term + weights[local].reshape(-1, 1) * back.reshape(-1, piece_width).astype(
                jnp.float32
            )
        outs.append(ring_reduce_scatter(term.astype(jnp.bfloat16), groups))
    ffn_out = jnp.concatenate(outs, axis=1)
    layer_out = (residual.astype(jnp.float32) + ffn_out).astype(jnp.bfloat16)
    return (layer_out, kv_pages)


def solution(mesh):
    placed = (
        P(("dp", "tensor"), None),
        P("dp"),
        P(),
        P(None, "tensor"),
        P(None, "tensor"),
        P(None, "tensor"),
        P("tensor", None),
        P(),
        P(None, "tensor"),
        P(None, "tensor"),
        P("tensor", None),
        P("tensor", None, None),
        P("tensor", None, None),
        P("tensor", None, None),
        P("dp", None),
        P("dp", None),
        P("dp"),
    )
    return jax.shard_map(
        shards,
        mesh=mesh,
        in_specs=placed,
        out_specs=(P(("dp", "tensor"), None), P(None, "dp", None, "tensor")),
        check_vma=False,
    )
```

```python
import jax
import jax.numpy as jnp
from jax import lax
from jax.sharding import PartitionSpec as P

HD = 128
TOP = 6
PAGE = 128


def rms_scale(hidden, gain):
    widened = hidden.astype(jnp.float32)
    inverse = lax.rsqrt(jnp.mean(widened * widened, axis=-1, keepdims=True) + 1e-06)
    return (widened * inverse * gain).astype(jnp.bfloat16)


def attend(projected, segment_ids, head_count):
    total_tokens = projected.shape[0]
    inner = head_count * HD
    queries = projected[:, :inner].reshape(total_tokens, head_count, HD)
    keys = projected[:, inner : 2 * inner].reshape(total_tokens, head_count, HD)
    values = projected[:, 2 * inner :].reshape(total_tokens, head_count, HD)
    scale = HD ** (-0.5)
    positions = jnp.arange(total_tokens, dtype=jnp.int32)
    span = min(512, total_tokens)

    def one_block(start):
        query_rows = lax.dynamic_slice_in_dim(queries, start, span, 0)
        query_segments = lax.dynamic_slice_in_dim(segment_ids, start, span, 0)
        query_positions = start + jnp.arange(span, dtype=jnp.int32)
        scores = (
            jnp.einsum("qhd,khd->hqk", query_rows, keys, preferred_element_type=jnp.float32) * scale
        )
        allowed = (query_segments[:, None] == segment_ids[None, :]) & (
            positions[None, :] <= query_positions[:, None]
        )
        scores = jnp.where(allowed[None], scores, -jnp.inf)
        highest = jnp.max(scores, axis=-1, keepdims=True)
        weights = jnp.exp(scores - highest)
        probs = (weights / jnp.sum(weights, axis=-1, keepdims=True)).astype(jnp.bfloat16)
        context = jnp.einsum("hqk,khd->qhd", probs, values, preferred_element_type=jnp.float32)
        return context.astype(jnp.bfloat16)

    starts = jnp.arange(total_tokens // span, dtype=jnp.int32) * span
    context = lax.map(one_block, starts).reshape(total_tokens, inner)
    return (context, keys.reshape(total_tokens, inner), values.reshape(total_tokens, inner))


def expert_apply(picked, gate_w, up_w, down_w):
    gate_part = jnp.dot(picked, gate_w, preferred_element_type=jnp.float32)
    upward = jnp.dot(picked, up_w, preferred_element_type=jnp.float32)
    hidden = (jax.nn.silu(gate_part) * upward).astype(jnp.bfloat16)
    return jnp.dot(hidden, down_w, preferred_element_type=jnp.float32).astype(jnp.bfloat16)


def ring_reduce_scatter(partial, groups):
    ring = groups // 4
    rows = partial.shape[0] // groups
    width = partial.shape[1]
    me = lax.axis_index("tensor")
    y = me // 4
    side = (me // 2) % 2
    core = me % 2
    blocks = partial.reshape(ring, 2, 2, rows, width)
    core_pairs = [(t, t ^ 1) for t in range(groups)]
    keep = lax.dynamic_index_in_dim(blocks, core, axis=2, keepdims=False)
    give = lax.dynamic_index_in_dim(blocks, 1 - core, axis=2, keepdims=False)
    got = lax.ppermute(give, "tensor", core_pairs)
    summed = keep.astype(jnp.float32) + got.astype(jnp.float32)
    half = width // 2
    forward_part = summed[..., :half]
    backward_part = summed[..., half:]
    forward_pairs = [(t, ((t // 4 + 1) % ring) * 4 + t % 4) for t in range(groups)]
    backward_pairs = [(t, ((t // 4 + ring - 1) % ring) * 4 + t % 4) for t in range(groups)]
    carry_f = lax.dynamic_index_in_dim(forward_part, (y + ring - 1) % ring, 0, False)
    carry_b = lax.dynamic_index_in_dim(backward_part, (y + 1) % ring, 0, False)
    carry_f = carry_f.astype(jnp.bfloat16)
    carry_b = carry_b.astype(jnp.bfloat16)
    for step in range(ring - 1):
        recv_f = lax.ppermute(carry_f, "tensor", forward_pairs)
        recv_b = lax.ppermute(carry_b, "tensor", backward_pairs)
        index_f = (y + 2 * ring - step - 2) % ring
        index_b = (y + step + 2) % ring
        acc_f = recv_f.astype(jnp.float32) + lax.dynamic_index_in_dim(
            forward_part, index_f, 0, False
        )
        acc_b = recv_b.astype(jnp.float32) + lax.dynamic_index_in_dim(
            backward_part, index_b, 0, False
        )
        carry_f = acc_f.astype(jnp.bfloat16)
        carry_b = acc_b.astype(jnp.bfloat16)
    mine = jnp.concatenate([acc_f, acc_b], axis=-1)
    side_pairs = [(t, t ^ 2) for t in range(groups)]
    keep_side = lax.dynamic_index_in_dim(mine, side, 0, False)
    give_side = lax.dynamic_index_in_dim(mine, 1 - side, 0, False).astype(jnp.bfloat16)
    got_side = lax.ppermute(give_side, "tensor", side_pairs)
    return keep_side + got_side.astype(jnp.float32)


def shards(
    tokens,
    segment_ids,
    attention_gain,
    query_weight,
    key_weight,
    value_weight,
    output_weight,
    ffn_gain,
    shared_gate,
    shared_up,
    shared_down,
    expert_gate,
    expert_up,
    expert_down,
    expert_ids,
    gate_weights,
    page_table,
):
    tok_dev = tokens.shape[0]
    groups = lax.axis_size("tensor")
    position = lax.axis_index("tensor")
    inner = query_weight.shape[1]
    head_count = inner // HD
    model_width = tokens.shape[1]

    projection = jnp.concatenate([query_weight, key_weight, value_weight], axis=1)
    normed_all = lax.all_gather(rms_scale(tokens, attention_gain), "tensor", axis=0, tiled=True)
    out_weight_all = lax.all_gather(output_weight, "tensor", axis=0, tiled=True)
    projected = lax.map(
        lambda rows: jnp.dot(rows, projection, preferred_element_type=jnp.float32).astype(
            jnp.bfloat16
        ),
        normed_all.reshape(4, -1, normed_all.shape[1]),
    ).reshape(normed_all.shape[0], -1)
    context, keys, values = attend(projected, segment_ids, head_count)
    cache = jnp.stack([keys, values]).reshape(2, -1, PAGE, inner)
    kv_pages = jnp.zeros_like(cache).at[:, page_table].set(cache)

    received = lax.all_to_all(
        context.reshape(groups, tok_dev, inner), "tensor", split_axis=0, concat_axis=0, tiled=True
    )
    context_rows = received.transpose(1, 0, 2).reshape(tok_dev, groups * inner)
    attention = jnp.dot(context_rows, out_weight_all, preferred_element_type=jnp.float32)
    residual = (tokens.astype(jnp.float32) + attention).astype(jnp.bfloat16)
    normed_ffn = rms_scale(residual, ffn_gain)
    piece_edges = [0, model_width * 5 // 8, model_width]
    normed_stream = lax.all_gather(normed_ffn, "tensor", axis=0, tiled=True)

    local_experts = expert_gate.shape[0]
    expert_count = local_experts * groups
    capacity = tok_dev * TOP // expert_count + tok_dev // 8
    id_blocks = expert_ids.reshape(groups, tok_dev, -1)
    gate_blocks = gate_weights.reshape(groups, tok_dev, -1)
    slots = jnp.arange(capacity, dtype=jnp.int32)
    onehots = []
    weights = []
    for local in range(local_experts):
        expert = position * local_experts + local
        chosen = id_blocks == expert
        hits = jnp.sum(chosen.astype(jnp.int32), axis=2)
        weights.append(jnp.sum(jnp.where(chosen, gate_blocks, 0.0), axis=2))
        rank = jnp.cumsum(hits, axis=1) - hits
        onehots.append(
            ((hits[:, None, :] > 0) & (rank[:, None, :] == slots[None, :, None])).astype(
                jnp.bfloat16
            )
        )

    shared_columns = jnp.concatenate([shared_gate, shared_up], axis=1)
    shared_width = shared_gate.shape[1]
    joined = jnp.dot(normed_stream, shared_columns, preferred_element_type=jnp.float32)
    token_blocks = normed_stream.reshape(groups, tok_dev, model_width)
    expert_gate_parts = []
    expert_up_parts = []
    for local in range(local_experts):
        picked = jnp.einsum(
            "bst,btd->bsd", onehots[local], token_blocks, preferred_element_type=jnp.float32
        ).astype(jnp.bfloat16).reshape(-1, model_width)
        expert_gate_parts.append(
            jnp.dot(picked, expert_gate[local], preferred_element_type=jnp.float32)
        )
        expert_up_parts.append(jnp.dot(picked, expert_up[local], preferred_element_type=jnp.float32))
    hidden_all = (jax.nn.silu(joined[:, :shared_width]) * joined[:, shared_width:]).astype(
        jnp.bfloat16
    )
    expert_hidden = [
        (jax.nn.silu(expert_gate_parts[local]) * expert_up_parts[local]).astype(jnp.bfloat16)
        for local in range(local_experts)
    ]

    outs = []
    for k in range(len(piece_edges) - 1):
        columns = slice(piece_edges[k], piece_edges[k + 1])
        piece_width = piece_edges[k + 1] - piece_edges[k]
        term = jnp.dot(hidden_all, shared_down[:, columns], preferred_element_type=jnp.float32)
        for local in range(local_experts):
            rows = jnp.dot(
                expert_hidden[local], expert_down[local][:, columns], preferred_element_type=jnp.float32
            ).astype(jnp.bfloat16)
            back = jnp.einsum(
                "bst,bsd->btd",
                onehots[local],
                rows.reshape(groups, capacity, piece_width),
                preferred_element_type=jnp.float32,
            ).astype(jnp.bfloat16)
            term = term + weights[local].reshape(-1, 1) * back.reshape(-1, piece_width).astype(
                jnp.float32
            )
        outs.append(ring_reduce_scatter(term.astype(jnp.bfloat16), groups))
    ffn_out = jnp.concatenate(outs, axis=1)
    layer_out = (residual.astype(jnp.float32) + ffn_out).astype(jnp.bfloat16)
    return (layer_out, kv_pages)


def solution(mesh):
    placed = (
        P(("dp", "tensor"), None),
        P("dp"),
        P(),
        P(None, "tensor"),
        P(None, "tensor"),
        P(None, "tensor"),
        P("tensor", None),
        P(),
        P(None, "tensor"),
        P(None, "tensor"),
        P("tensor", None),
        P("tensor", None, None),
        P("tensor", None, None),
        P("tensor", None, None),
        P("dp", None),
        P("dp", None),
        P("dp"),
    )
    return jax.shard_map(
        shards,
        mesh=mesh,
        in_specs=placed,
        out_specs=(P(("dp", "tensor"), None), P(None, "dp", None, "tensor")),
        check_vma=False,
    )
```

```python
import jax
import jax.numpy as jnp
from jax import lax
from jax.sharding import PartitionSpec as P

HD = 128
TOP = 6
PAGE = 128


def rms_scale(hidden, gain):
    widened = hidden.astype(jnp.float32)
    inverse = lax.rsqrt(jnp.mean(widened * widened, axis=-1, keepdims=True) + 1e-06)
    return (widened * inverse * gain).astype(jnp.bfloat16)


def attend(projected, segment_ids, head_count):
    total_tokens = projected.shape[0]
    inner = head_count * HD
    queries = projected[:, :inner].reshape(total_tokens, head_count, HD)
    keys = projected[:, inner : 2 * inner].reshape(total_tokens, head_count, HD)
    values = projected[:, 2 * inner :].reshape(total_tokens, head_count, HD)
    scale = HD ** (-0.5)
    positions = jnp.arange(total_tokens, dtype=jnp.int32)
    span = min(512, total_tokens)

    def one_block(start):
        query_rows = lax.dynamic_slice_in_dim(queries, start, span, 0)
        query_segments = lax.dynamic_slice_in_dim(segment_ids, start, span, 0)
        query_positions = start + jnp.arange(span, dtype=jnp.int32)
        scores = (
            jnp.einsum("qhd,khd->hqk", query_rows, keys, preferred_element_type=jnp.float32) * scale
        )
        allowed = (query_segments[:, None] == segment_ids[None, :]) & (
            positions[None, :] <= query_positions[:, None]
        )
        scores = jnp.where(allowed[None], scores, -jnp.inf)
        highest = jnp.max(scores, axis=-1, keepdims=True)
        weights = jnp.exp(scores - highest)
        probs = (weights / jnp.sum(weights, axis=-1, keepdims=True)).astype(jnp.bfloat16)
        context = jnp.einsum("hqk,khd->qhd", probs, values, preferred_element_type=jnp.float32)
        return context.astype(jnp.bfloat16)

    starts = jnp.arange(total_tokens // span, dtype=jnp.int32) * span
    context = lax.map(one_block, starts).reshape(total_tokens, inner)
    return (context, keys.reshape(total_tokens, inner), values.reshape(total_tokens, inner))


def expert_apply(picked, gate_w, up_w, down_w):
    gate_part = jnp.dot(picked, gate_w, preferred_element_type=jnp.float32)
    upward = jnp.dot(picked, up_w, preferred_element_type=jnp.float32)
    hidden = (jax.nn.silu(gate_part) * upward).astype(jnp.bfloat16)
    return jnp.dot(hidden, down_w, preferred_element_type=jnp.float32).astype(jnp.bfloat16)


def ring_reduce_scatter(partial, groups):
    ring = groups // 4
    rows = partial.shape[0] // groups
    width = partial.shape[1]
    me = lax.axis_index("tensor")
    y = me // 4
    side = (me // 2) % 2
    core = me % 2
    blocks = partial.reshape(ring, 2, 2, rows, width)
    core_pairs = [(t, t ^ 1) for t in range(groups)]
    keep = lax.dynamic_index_in_dim(blocks, core, axis=2, keepdims=False)
    give = lax.dynamic_index_in_dim(blocks, 1 - core, axis=2, keepdims=False)
    got = lax.ppermute(give, "tensor", core_pairs)
    summed = keep.astype(jnp.float32) + got.astype(jnp.float32)
    half = width // 2
    forward_part = summed[..., :half]
    backward_part = summed[..., half:]
    forward_pairs = [(t, ((t // 4 + 1) % ring) * 4 + t % 4) for t in range(groups)]
    backward_pairs = [(t, ((t // 4 + ring - 1) % ring) * 4 + t % 4) for t in range(groups)]
    carry_f = lax.dynamic_index_in_dim(forward_part, (y + ring - 1) % ring, 0, False)
    carry_b = lax.dynamic_index_in_dim(backward_part, (y + 1) % ring, 0, False)
    carry_f = carry_f.astype(jnp.bfloat16)
    carry_b = carry_b.astype(jnp.bfloat16)
    for step in range(ring - 1):
        recv_f = lax.ppermute(carry_f, "tensor", forward_pairs)
        recv_b = lax.ppermute(carry_b, "tensor", backward_pairs)
        index_f = (y + 2 * ring - step - 2) % ring
        index_b = (y + step + 2) % ring
        acc_f = recv_f.astype(jnp.float32) + lax.dynamic_index_in_dim(
            forward_part, index_f, 0, False
        )
        acc_b = recv_b.astype(jnp.float32) + lax.dynamic_index_in_dim(
            backward_part, index_b, 0, False
        )
        carry_f = acc_f.astype(jnp.bfloat16)
        carry_b = acc_b.astype(jnp.bfloat16)
    mine = jnp.concatenate([acc_f, acc_b], axis=-1)
    side_pairs = [(t, t ^ 2) for t in range(groups)]
    keep_side = lax.dynamic_index_in_dim(mine, side, 0, False)
    give_side = lax.dynamic_index_in_dim(mine, 1 - side, 0, False).astype(jnp.bfloat16)
    got_side = lax.ppermute(give_side, "tensor", side_pairs)
    return keep_side + got_side.astype(jnp.float32)


def shards(
    tokens,
    segment_ids,
    attention_gain,
    query_weight,
    key_weight,
    value_weight,
    output_weight,
    ffn_gain,
    shared_gate,
    shared_up,
    shared_down,
    expert_gate,
    expert_up,
    expert_down,
    expert_ids,
    gate_weights,
    page_table,
):
    tok_dev = tokens.shape[0]
    groups = lax.axis_size("tensor")
    position = lax.axis_index("tensor")
    inner = query_weight.shape[1]
    head_count = inner // HD
    model_width = tokens.shape[1]

    projection = jnp.concatenate([query_weight, key_weight, value_weight], axis=1)
    normed_all = lax.all_gather(rms_scale(tokens, attention_gain), "tensor", axis=0, tiled=True)
    out_weight_all = lax.all_gather(output_weight, "tensor", axis=0, tiled=True)
    projected = lax.map(
        lambda rows: jnp.dot(rows, projection, preferred_element_type=jnp.float32).astype(
            jnp.bfloat16
        ),
        normed_all.reshape(4, -1, normed_all.shape[1]),
    ).reshape(normed_all.shape[0], -1)
    context, keys, values = attend(projected, segment_ids, head_count)
    cache = jnp.stack([keys, values]).reshape(2, -1, PAGE, inner)
    kv_pages = jnp.zeros_like(cache).at[:, page_table].set(cache)

    received = lax.all_to_all(
        context.reshape(groups, tok_dev, inner), "tensor", split_axis=0, concat_axis=0, tiled=True
    )
    context_rows = received.transpose(1, 0, 2).reshape(tok_dev, groups * inner)
    attention = jnp.dot(context_rows, out_weight_all, preferred_element_type=jnp.float32)
    residual = (tokens.astype(jnp.float32) + attention).astype(jnp.bfloat16)
    normed_ffn = rms_scale(residual, ffn_gain)
    piece_edges = [0, model_width * 3 // 8, model_width]
    normed_stream = lax.all_gather(normed_ffn, "tensor", axis=0, tiled=True)

    local_experts = expert_gate.shape[0]
    expert_count = local_experts * groups
    capacity = tok_dev * TOP // expert_count + tok_dev // 8
    id_blocks = expert_ids.reshape(groups, tok_dev, -1)
    gate_blocks = gate_weights.reshape(groups, tok_dev, -1)
    slots = jnp.arange(capacity, dtype=jnp.int32)
    onehots = []
    weights = []
    for local in range(local_experts):
        expert = position * local_experts + local
        chosen = id_blocks == expert
        hits = jnp.sum(chosen.astype(jnp.int32), axis=2)
        weights.append(jnp.sum(jnp.where(chosen, gate_blocks, 0.0), axis=2))
        rank = jnp.cumsum(hits, axis=1) - hits
        onehots.append(
            ((hits[:, None, :] > 0) & (rank[:, None, :] == slots[None, :, None])).astype(
                jnp.bfloat16
            )
        )

    shared_columns = jnp.concatenate([shared_gate, shared_up], axis=1)
    shared_width = shared_gate.shape[1]
    joined = jnp.dot(normed_stream, shared_columns, preferred_element_type=jnp.float32)
    token_blocks = normed_stream.reshape(groups, tok_dev, model_width)
    expert_gate_parts = []
    expert_up_parts = []
    for local in range(local_experts):
        picked = jnp.einsum(
            "bst,btd->bsd", onehots[local], token_blocks, preferred_element_type=jnp.float32
        ).astype(jnp.bfloat16).reshape(-1, model_width)
        expert_gate_parts.append(
            jnp.dot(picked, expert_gate[local], preferred_element_type=jnp.float32)
        )
        expert_up_parts.append(jnp.dot(picked, expert_up[local], preferred_element_type=jnp.float32))
    hidden_all = (jax.nn.silu(joined[:, :shared_width]) * joined[:, shared_width:]).astype(
        jnp.bfloat16
    )
    expert_hidden = [
        (jax.nn.silu(expert_gate_parts[local]) * expert_up_parts[local]).astype(jnp.bfloat16)
        for local in range(local_experts)
    ]

    outs = []
    for k in range(len(piece_edges) - 1):
        columns = slice(piece_edges[k], piece_edges[k + 1])
        piece_width = piece_edges[k + 1] - piece_edges[k]
        term = jnp.dot(hidden_all, shared_down[:, columns], preferred_element_type=jnp.float32)
        for local in range(local_experts):
            rows = jnp.dot(
                expert_hidden[local], expert_down[local][:, columns], preferred_element_type=jnp.float32
            ).astype(jnp.bfloat16)
            back = jnp.einsum(
                "bst,bsd->btd",
                onehots[local],
                rows.reshape(groups, capacity, piece_width),
                preferred_element_type=jnp.float32,
            ).astype(jnp.bfloat16)
            term = term + weights[local].reshape(-1, 1) * back.reshape(-1, piece_width).astype(
                jnp.float32
            )
        outs.append(ring_reduce_scatter(term.astype(jnp.bfloat16), groups))
    ffn_out = jnp.concatenate(outs, axis=1)
    layer_out = (residual.astype(jnp.float32) + ffn_out).astype(jnp.bfloat16)
    return (layer_out, kv_pages)


def solution(mesh):
    placed = (
        P(("dp", "tensor"), None),
        P("dp"),
        P(),
        P(None, "tensor"),
        P(None, "tensor"),
        P(None, "tensor"),
        P("tensor", None),
        P(),
        P(None, "tensor"),
        P(None, "tensor"),
        P("tensor", None),
        P("tensor", None, None),
        P("tensor", None, None),
        P("tensor", None, None),
        P("dp", None),
        P("dp", None),
        P("dp"),
    )
    return jax.shard_map(
        shards,
        mesh=mesh,
        in_specs=placed,
        out_specs=(P(("dp", "tensor"), None), P(None, "dp", None, "tensor")),
        check_vma=False,
    )
```
